32 devices in a mesh: groups: 2 (over y), chan: 4 (over z), tm: 4 (over x, core).
Axes of the slice: x: 2, y: 2, z: 4, core: 2. Of those that a mesh axis runs over, the one named last changes fastest.
Arguments:
- samples: bfloat16 [2, 16, 1024, 4096], P(None, None, ('groups', 'chan'), 'tm'), parts along dimension 2, may hold values from -6 to 6
- station_gain: float32 [1024], P(('groups', 'chan')), parts along dimension 0, may hold values from 0.5 to 4
- station_map: int32 [1024], P('groups'), parts along dimension 0, may hold values from 0 to 511, each once
- steer_phase: float32 [16, 512, 1024], P('chan', None, ('groups', 'tm')), parts along dimension 2, may hold values from -3.140625 to 3.140625
Outputs:
- beams_out: bfloat16 [16, 4096, 2, 1024], P('chan', 'tm', None, 'groups'), parts along dimension 3
The draws below stay inside these ranges and needn't reach their ends.
There are 2 independent parts, one for each index of `groups`. The reference program is written for one: setup_inputs(seed, part) draws one part's arguments, and reference() takes and returns one part's arrays. A program takes and returns all parts, laid end to end along the dimension named above; each array names one. Nothing has to cross between parts.
Inputs may be any that keep to these rules, and one draw needn't show every extreme that they name: station_map names each of the 512 stations once.
All inputs are finite; a program needn't handle non-finite values.
Results may differ from the reference program's by a relative error of at most 0.015.
Values may be sent and summed in bfloat16 or wider, within the bound.
No kernel may reach another device: no remote copies, remote signals or barrier semaphores. Data moves between devices by JAX's collectives and lax.ppermute only.
A program may use at most 256 MiB of HBM per device.

```python
import math
import jax
import jax.numpy as jnp
from jax import lax

S = 512
F = 16
BEAMS = 512
ITERS = 8
SPECTRA = 4096


def block_scale(stream_key, extent, split, low, high):
    loudness, own = 1.0, jax.random.fold_in(stream_key, 6)
    for axis_at, blocks in split:
        draws = jnp.exp(jax.random.uniform(jax.random.fold_in(own, axis_at), (blocks,), jnp.float32, low / len(split), high / len(split)))
        loudness = loudness * jnp.repeat(draws, extent[axis_at] // blocks).reshape([-1 if axis == axis_at else 1 for axis in range(len(extent))])
    return loudness


def bell_draw(rng, dims, scale, limit, split=(), kind=jnp.bfloat16):
    values = scale * jax.random.normal(rng, dims, jnp.float32)
    if split:
        values = values * block_scale(rng, dims, split, -0.22, 0.18)
    return jnp.clip(values, -limit, limit).astype(kind)


def setup_inputs(seed: int = 0, part: int = 0) -> dict:
    arg_keys = jax.random.split(jax.random.key(seed), 5)
    part_splits = jax.random.split(jax.random.fold_in(arg_keys[4], part), 5)
    return {
        "samples": bell_draw(part_splits[0], (2, F, S, SPECTRA), 1.0, 6.0, ((2, 4), (3, 4))),
        "station_gain": jnp.clip(jnp.exp(math.log(4.0) - 2.0794415 * jax.random.uniform(part_splits[1], (S,), jnp.float32) ** block_scale(part_splits[1], (S,), ((0, 4),), -0.2, 0.2)), 0.5, 4.0),
        "station_map": jax.random.permutation(part_splits[2], S).astype(jnp.int32),
        "steer_phase": jnp.clip(jax.random.uniform(part_splits[3], (F, S, BEAMS), jnp.float32, -3.140625, 3.140625), -3.140625, 3.140625),
    }


def dft_table(count):
    index = jnp.arange(count, dtype=jnp.int32)
    turns = (index[:, None] * index[None, :] % count).astype(jnp.float32)
    angle_grid = 2.0 * math.pi * turns / count
    cosine = jnp.cos(angle_grid)
    sine = jnp.sin(angle_grid)
    upper = jnp.concatenate((cosine, sine), axis=1)
    lower = jnp.concatenate((-sine, cosine), axis=1)
    return jnp.concatenate((upper, lower), axis=0).astype(jnp.bfloat16)

def solve_channel(cov_real, cov_imag, loading, center, radius, steer_real, steer_imag):
    high = lax.Precision.HIGHEST

    def apply_op(vec_real, vec_imag):
        out_real = jnp.dot(cov_real, vec_real, precision=high) - jnp.dot(cov_imag, vec_imag, precision=high)
        out_imag = jnp.dot(cov_imag, vec_real, precision=high) + jnp.dot(cov_real, vec_imag, precision=high)
        return (out_real + loading * vec_real, out_imag + loading * vec_imag)
    sol_real = jnp.zeros_like(steer_real)
    sol_imag = jnp.zeros_like(steer_imag)
    res_real, res_imag = (steer_real, steer_imag)
    dir_real = res_real / center
    dir_imag = res_imag / center
    rho_prev = radius / center
    for iteration in range(ITERS):
        sol_real = sol_real + dir_real
        sol_imag = sol_imag + dir_imag
        img_real, img_imag = apply_op(dir_real, dir_imag)
        res_real = res_real - img_real
        res_imag = res_imag - img_imag
        rho_next = 1.0 / (2.0 * center / radius - rho_prev)
        dir_real = rho_next * rho_prev * dir_real + 2.0 * rho_next / radius * res_real
        dir_imag = rho_next * rho_prev * dir_imag + 2.0 * rho_next / radius * res_imag
        rho_prev = rho_next
    return (sol_real, sol_imag)

def reference(samples, station_gain, station_map, steer_phase):
    count = samples.shape[1]
    stations = samples.shape[2]
    spectra_count = samples.shape[3]
    channelized = jnp.dot(dft_table(count), samples.reshape(2 * count, -1), preferred_element_type=jnp.float32)
    channelized = channelized.reshape(2, count, stations, spectra_count)
    spectra = (channelized * station_gain[None, None, :, None]).astype(jnp.bfloat16)

    def one_channel(channel):
        stacked = jnp.concatenate((spectra[0, channel], spectra[1, channel]), axis=0).astype(jnp.float32)
        gram_sum = jnp.dot(stacked, stacked.T, precision=lax.Precision.HIGHEST)
        cov_real = (gram_sum[:stations, :stations] + gram_sum[stations:, stations:]) / spectra_count
        cov_imag = (gram_sum[stations:, :stations] - gram_sum[:stations, stations:]) / spectra_count
        loading = jnp.sum(jnp.diagonal(cov_real)) / stations
        row_mass = lax.optimization_barrier(jnp.sum(jnp.sqrt(cov_real * cov_real + cov_imag * cov_imag), axis=1))
        bound = loading + jnp.max(row_mass)
        center = (bound + loading) / 2.0
        radius = (bound - loading) / 2.0
        phase_rows = jnp.take(steer_phase[channel], station_map, axis=0)
        steer_real = jnp.cos(phase_rows)
        steer_imag = jnp.sin(phase_rows)
        sol_real, sol_imag = solve_channel(cov_real, cov_imag, loading, center, radius, steer_real, steer_imag)
        response = lax.optimization_barrier(jnp.sum(steer_real * sol_real + steer_imag * sol_imag, axis=0, keepdims=True))
        weight_real = (sol_real / response).astype(jnp.bfloat16)
        weight_imag = (sol_imag / response).astype(jnp.bfloat16)
        weight_cat = jnp.stack((jnp.concatenate((weight_real, weight_imag), axis=0), jnp.concatenate((-weight_imag, weight_real), axis=0)), axis=1)
        formed = jnp.dot(stacked.T, weight_cat.astype(jnp.float32).reshape(2 * stations, -1), precision=lax.Precision.HIGHEST)
        return formed.reshape(spectra_count, 2, -1).astype(jnp.bfloat16)
    return lax.map(one_channel, jnp.arange(count, dtype=jnp.int32))
```

```python
import math

import jax
import jax.numpy as jnp
from jax import lax
from jax.sharding import PartitionSpec as P

ITERS = 8


def dft_table(count):
    index = jnp.arange(count, dtype=jnp.int32)
    turns = (index[:, None] * index[None, :] % count).astype(jnp.float32)
    angle_grid = 2.0 * math.pi * turns / count
    cosine = jnp.cos(angle_grid)
    sine = jnp.sin(angle_grid)
    upper = jnp.concatenate((cosine, sine), axis=1)
    lower = jnp.concatenate((-sine, cosine), axis=1)
    table = jnp.concatenate((upper, lower), axis=0).astype(jnp.bfloat16)
    return table.reshape(2, count, 2 * count).transpose(1, 0, 2).reshape(2 * count, 2 * count)


def chebyshev(cov_real, cov_imag, steer_real, steer_imag):
    high = lax.Precision.HIGHEST
    stations = cov_real.shape[1]
    loading = jnp.sum(jnp.diagonal(cov_real, axis1=1, axis2=2), axis=1) / stations
    row_mass = jnp.sum(jnp.sqrt(cov_real * cov_real + cov_imag * cov_imag), axis=2)
    bound = loading + jnp.max(row_mass, axis=1)
    center = ((bound + loading) / 2.0)[:, None, None]
    radius = ((bound - loading) / 2.0)[:, None, None]
    eye = jnp.eye(stations, dtype=jnp.float32)
    loaded = cov_real + loading[:, None, None] * eye
    block = jnp.concatenate(
        (
            jnp.concatenate((loaded, -cov_imag), axis=2),
            jnp.concatenate((cov_imag, loaded), axis=2),
        ),
        axis=1,
    )
    steer = jnp.concatenate((steer_real, steer_imag), axis=1)
    res = steer
    dirn = res / center
    sol = jnp.zeros_like(steer)
    rho = radius / center

    def body(_, carry):
        sol, res, dirn, rho = carry
        sol = sol + dirn
        img = jnp.einsum("cjk,ckb->cjb", block, dirn, precision=high)
        res = res - img
        rho_next = 1.0 / (2.0 * center / radius - rho)
        dirn = rho_next * rho * dirn + 2.0 * rho_next / radius * res
        return sol, res, dirn, rho_next

    sol, _, _, _ = lax.fori_loop(0, ITERS, body, (sol, res, dirn, rho))
    response = jnp.sum(steer * sol, axis=1, keepdims=True)
    weights = (sol / response).astype(jnp.bfloat16)
    return weights.reshape(weights.shape[0], 2, stations, weights.shape[2])


def local(samples, station_gain, station_map, steer_phase):
    count = samples.shape[1]
    row_count = samples.shape[2]
    spec_count = samples.shape[3]
    chan_size = lax.axis_size("chan")
    tm_size = lax.axis_size("tm")
    channelized = jnp.dot(
        dft_table(count), samples.reshape(2 * count, -1), preferred_element_type=jnp.float32
    )
    channelized = channelized.reshape(count, 2, row_count, spec_count)
    spectra = (channelized * station_gain[None, None, :, None]).astype(jnp.bfloat16)
    owned = lax.all_to_all(spectra, "chan", split_axis=0, concat_axis=2, tiled=True)
    chans = owned.shape[0]
    stations = owned.shape[2]
    stacked = owned.reshape(chans, 2 * stations, spec_count)
    spectra_total = spec_count * tm_size
    gram_sum = jnp.einsum("cat,cbt->cab", stacked, stacked, preferred_element_type=jnp.float32)
    part_real = gram_sum[:, :stations, :stations] + gram_sum[:, stations:, stations:]
    part_imag = gram_sum[:, stations:, :stations] - gram_sum[:, :stations, stations:]
    part = jnp.stack((part_real, part_imag), axis=1).astype(jnp.bfloat16)
    if chans % tm_size == 0:
        cov = lax.psum_scatter(part, "tm", scatter_dimension=0, tiled=True).astype(jnp.float32)
        phase = lax.all_to_all(steer_phase, "tm", split_axis=0, concat_axis=2, tiled=True)
    else:
        cov = lax.psum(part, "tm").astype(jnp.float32)
        phase = steer_phase
    cov = cov / spectra_total
    phase_rows = jnp.take(phase, station_map, axis=1)
    weights = chebyshev(cov[:, 0], cov[:, 1], jnp.cos(phase_rows), jnp.sin(phase_rows))
    if chans % tm_size == 0:
        weights = lax.all_gather(weights, "tm", axis=0, tiled=True)
    else:
        weights = lax.all_gather(weights, "tm", axis=3, tiled=True)
    weight_real = weights[:, 0]
    weight_imag = weights[:, 1]
    weight_cat = jnp.stack(
        (
            jnp.concatenate((weight_real, weight_imag), axis=1),
            jnp.concatenate((-weight_imag, weight_real), axis=1),
        ),
        axis=2,
    )
    formed = jnp.einsum("cat,cakb->ctkb", stacked, weight_cat, preferred_element_type=jnp.float32)
    return formed.astype(jnp.bfloat16)


def solution(mesh):
    in_specs = (
        P(None, None, ("groups", "chan"), "tm"),
        P(("groups", "chan")),
        P("groups"),
        P("chan", None, ("groups", "tm")),
    )
    out_specs = P("chan", "tm", None, "groups")
    return jax.shard_map(local, mesh=mesh, in_specs=in_specs, out_specs=out_specs, check_vma=False)
```

```python
import math

import jax
import jax.numpy as jnp
from jax import lax
from jax.sharding import PartitionSpec as P

ITERS = 8


def dft_table(count):
    index = jnp.arange(count, dtype=jnp.int32)
    turns = (index[:, None] * index[None, :] % count).astype(jnp.float32)
    angle_grid = 2.0 * math.pi * turns / count
    cosine = jnp.cos(angle_grid)
    sine = jnp.sin(angle_grid)
    upper = jnp.concatenate((cosine, sine), axis=1)
    lower = jnp.concatenate((-sine, cosine), axis=1)
    table = jnp.concatenate((upper, lower), axis=0).astype(jnp.bfloat16)
    return table.reshape(2, count, 2 * count).transpose(1, 0, 2).reshape(2 * count, 2 * count)


def chebyshev(cov_real, cov_imag, steer_real, steer_imag):
    high = lax.Precision.HIGH
    stations = cov_real.shape[1]
    loading = jnp.sum(jnp.diagonal(cov_real, axis1=1, axis2=2), axis=1) / stations
    row_mass = jnp.sum(jnp.sqrt(cov_real * cov_real + cov_imag * cov_imag), axis=2)
    bound = loading + jnp.max(row_mass, axis=1)
    center = ((bound + loading) / 2.0)[:, None, None]
    radius = ((bound - loading) / 2.0)[:, None, None]
    eye = jnp.eye(stations, dtype=jnp.float32)
    loaded = cov_real + loading[:, None, None] * eye
    block = jnp.concatenate(
        (
            jnp.concatenate((loaded, -cov_imag), axis=2),
            jnp.concatenate((cov_imag, loaded), axis=2),
        ),
        axis=1,
    )
    steer = jnp.concatenate((steer_real, steer_imag), axis=1)
    res = steer
    dirn = res / center
    sol = jnp.zeros_like(steer)
    rho = radius / center

    def body(_, carry):
        sol, res, dirn, rho = carry
        sol = sol + dirn
        img = jnp.einsum("cjk,ckb->cjb", block, dirn, precision=high)
        res = res - img
        rho_next = 1.0 / (2.0 * center / radius - rho)
        dirn = rho_next * rho * dirn + 2.0 * rho_next / radius * res
        return sol, res, dirn, rho_next

    sol, _, _, _ = lax.fori_loop(0, ITERS, body, (sol, res, dirn, rho))
    response = jnp.sum(steer * sol, axis=1, keepdims=True)
    weights = (sol / response).astype(jnp.bfloat16)
    return weights.reshape(weights.shape[0], 2, stations, weights.shape[2])


def exchange_phase(steer_phase, tm_size):
    own = lax.axis_index("tm")
    block = steer_phase.shape[0] // tm_size
    pieces = steer_phase.reshape(tm_size, block, *steer_phase.shape[1:])
    received = [lax.dynamic_index_in_dim(pieces, own, 0, keepdims=False)]
    for shift in range(1, tm_size):
        target = (own + shift) % tm_size
        outgoing = lax.dynamic_index_in_dim(pieces, target, 0, keepdims=False)
        perm = [(j, (j + shift) % tm_size) for j in range(tm_size)]
        received.append(lax.ppermute(outgoing, "tm", perm))
    stacked = jnp.stack(received, axis=0)
    order = (own - jnp.arange(tm_size)) % tm_size
    ordered = jnp.take(stacked, order, axis=0)
    return jnp.moveaxis(ordered, 0, 2).reshape(block, steer_phase.shape[1], -1)


def local(samples, station_gain, station_map, steer_phase):
    count = samples.shape[1]
    row_count = samples.shape[2]
    spec_count = samples.shape[3]
    chan_size = lax.axis_size("chan")
    tm_size = lax.axis_size("tm")
    channelized = jnp.dot(
        dft_table(count), samples.reshape(2 * count, -1), preferred_element_type=jnp.float32
    )
    channelized = channelized.reshape(count, 2, row_count, spec_count)
    spectra = (channelized * station_gain[None, None, :, None]).astype(jnp.bfloat16)
    split_channels = (count // chan_size) % tm_size == 0
    if split_channels:
        phase = exchange_phase(steer_phase, tm_size)
        spectra, phase = lax.optimization_barrier((spectra, phase))
    else:
        phase = steer_phase
    owned = lax.all_to_all(spectra, "chan", split_axis=0, concat_axis=2, tiled=True)
    chans = owned.shape[0]
    stations = owned.shape[2]
    stacked = owned.reshape(chans, 2 * stations, spec_count)
    spectra_total = spec_count * tm_size
    gram_sum = jnp.einsum("cat,cbt->cab", stacked, stacked, preferred_element_type=jnp.float32)
    part_real = gram_sum[:, :stations, :stations] + gram_sum[:, stations:, stations:]
    part_imag = gram_sum[:, stations:, :stations] - gram_sum[:, :stations, stations:]
    part = jnp.concatenate((part_real, part_imag), axis=1).astype(jnp.bfloat16)
    if split_channels:
        cov = lax.psum_scatter(part, "tm", scatter_dimension=0, tiled=True).astype(jnp.float32)
    else:
        cov = lax.psum(part, "tm").astype(jnp.float32)
    cov = cov / spectra_total
    phase_rows = jnp.take(phase, station_map, axis=1)
    weights = chebyshev(
        cov[:, :stations], cov[:, stations:], jnp.cos(phase_rows), jnp.sin(phase_rows)
    )
    if split_channels:
        weights = lax.all_gather(weights, "tm", axis=0, tiled=True)
    else:
        weights = lax.all_gather(weights, "tm", axis=3, tiled=True)
    weight_real = weights[:, 0]
    weight_imag = weights[:, 1]
    weight_cat = jnp.stack(
        (
            jnp.concatenate((weight_real, weight_imag), axis=1),
            jnp.concatenate((-weight_imag, weight_real), axis=1),
        ),
        axis=2,
    )
    formed = jnp.einsum("cat,cakb->ctkb", stacked, weight_cat, preferred_element_type=jnp.float32)
    return formed.astype(jnp.bfloat16)


def solution(mesh):
    in_specs = (
        P(None, None, ("groups", "chan"), "tm"),
        P(("groups", "chan")),
        P("groups"),
        P("chan", None, ("groups", "tm")),
    )
    out_specs = P("chan", "tm", None, "groups")
    return jax.shard_map(local, mesh=mesh, in_specs=in_specs, out_specs=out_specs, check_vma=False)
```

```python
import math

import jax
import jax.numpy as jnp
from jax import lax
from jax.sharding import PartitionSpec as P

ITERS = 8


def full_dft_table(count):
    index = jnp.arange(count, dtype=jnp.int32)
    turns = (index[:, None] * index[None, :] % count).astype(jnp.float32)
    angle_grid = 2.0 * math.pi * turns / count
    cosine = jnp.cos(angle_grid)
    sine = jnp.sin(angle_grid)
    upper = jnp.concatenate((cosine, sine), axis=1)
    lower = jnp.concatenate((-sine, cosine), axis=1)
    return jnp.concatenate((upper, lower), axis=0).astype(jnp.bfloat16)


def chebyshev(cov_real, cov_imag, steer_real, steer_imag):
    high = lax.Precision.HIGH
    stations = cov_real.shape[1]
    loading = jnp.sum(jnp.diagonal(cov_real, axis1=1, axis2=2), axis=1) / stations
    row_mass = jnp.sum(jnp.sqrt(cov_real * cov_real + cov_imag * cov_imag), axis=2)
    bound = loading + jnp.max(row_mass, axis=1)
    center = ((bound + loading) / 2.0)[:, None, None]
    radius = ((bound - loading) / 2.0)[:, None, None]
    eye = jnp.eye(stations, dtype=jnp.float32)
    loaded = cov_real + loading[:, None, None] * eye
    block = jnp.concatenate(
        (
            jnp.concatenate((loaded, -cov_imag), axis=2),
            jnp.concatenate((cov_imag, loaded), axis=2),
        ),
        axis=1,
    )
    steer = jnp.concatenate((steer_real, steer_imag), axis=1)
    res = steer
    dirn = res / center
    sol = jnp.zeros_like(steer)
    rho = radius / center

    def body(_, carry):
        sol, res, dirn, rho = carry
        sol = sol + dirn
        img = jnp.einsum("cjk,ckb->cjb", block, dirn, precision=high)
        res = res - img
        rho_next = 1.0 / (2.0 * center / radius - rho)
        dirn = rho_next * rho * dirn + 2.0 * rho_next / radius * res
        return sol, res, dirn, rho_next

    sol, _, _, _ = lax.fori_loop(0, ITERS, body, (sol, res, dirn, rho))
    response = jnp.sum(steer * sol, axis=1, keepdims=True)
    weights = (sol / response).astype(jnp.bfloat16)
    return weights.reshape(weights.shape[0], 2, stations, weights.shape[2])


def local(samples, station_gain, station_map, steer_phase):
    count = samples.shape[1]
    row_count = samples.shape[2]
    spec_count = samples.shape[3]
    chan_size = lax.axis_size("chan")
    tm_size = lax.axis_size("tm")
    slots = count // chan_size
    here = lax.axis_index("chan")
    stations = chan_size * row_count
    spectra_total = spec_count * tm_size
    table = full_dft_table(count)
    flat = samples.reshape(2 * count, -1)
    gain = station_gain[None, None, :, None]
    source = (here - jnp.arange(chan_size)) % chan_size
    arrival = (source[:, None] * row_count + jnp.arange(row_count)[None, :]).reshape(-1)
    phase_rows = jnp.take(steer_phase, jnp.take(station_map, arrival), axis=1)
    steer_real = jnp.cos(phase_rows)
    steer_imag = jnp.sin(phase_rows)
    previous = None
    beams = []
    for slot in range(slots):
        rows = [part * count + dest * slots + slot for dest in range(chan_size) for part in range(2)]
        channelized = jnp.dot(table[jnp.array(rows)], flat, preferred_element_type=jnp.float32)
        channelized = channelized.reshape(chan_size, 2, row_count, spec_count)
        spectra = (channelized * gain).astype(jnp.bfloat16)
        if previous is not None:
            spectra, _ = lax.optimization_barrier((spectra, previous))
        received = [lax.dynamic_index_in_dim(spectra, here, 0, keepdims=False)]
        for shift in range(1, chan_size):
            outgoing = lax.dynamic_index_in_dim(spectra, (here + shift) % chan_size, 0, keepdims=False)
            perm = [(j, (j + shift) % chan_size) for j in range(chan_size)]
            received.append(lax.ppermute(outgoing, "chan", perm))
        previous = tuple(received)
        stacked = jnp.stack(received, axis=1).reshape(2 * stations, spec_count)
        gram_sum = jnp.dot(stacked, stacked.T, preferred_element_type=jnp.float32)
        part_real = gram_sum[:stations, :stations] + gram_sum[stations:, stations:]
        part_imag = gram_sum[stations:, :stations] - gram_sum[:stations, stations:]
        part = jnp.concatenate((part_real, part_imag), axis=0).astype(jnp.bfloat16)
        if slot > 0:
            part, _ = lax.optimization_barrier((part, reduced))
        reduced = lax.psum(part, "tm")
        cov = reduced.astype(jnp.float32) / spectra_total
        weights = chebyshev(
            cov[None, :stations],
            cov[None, stations:],
            steer_real[slot : slot + 1],
            steer_imag[slot : slot + 1],
        )
        weights = lax.all_gather(weights[0], "tm", axis=2, tiled=True)
        weight_real = weights[0]
        weight_imag = weights[1]
        weight_cat = jnp.stack(
            (
                jnp.concatenate((weight_real, weight_imag), axis=0),
                jnp.concatenate((-weight_imag, weight_real), axis=0),
            ),
            axis=1,
        )
        formed = jnp.einsum("at,akb->tkb", stacked, weight_cat, preferred_element_type=jnp.float32)
        beams.append(formed.astype(jnp.bfloat16))
    return jnp.stack(beams, axis=0)


def solution(mesh):
    in_specs = (
        P(None, None, ("groups", "chan"), "tm"),
        P(("groups", "chan")),
        P("groups"),
        P("chan", None, ("groups", "tm")),
    )
    out_specs = P("chan", "tm", None, "groups")
    return jax.shard_map(local, mesh=mesh, in_specs=in_specs, out_specs=out_specs, check_vma=False)
```

```python
import math

import jax
import jax.numpy as jnp
from jax import lax
from jax.sharding import PartitionSpec as P

ITERS = 8


def dft_table(count):
    index = jnp.arange(count, dtype=jnp.int32)
    turns = (index[:, None] * index[None, :] % count).astype(jnp.float32)
    angle_grid = 2.0 * math.pi * turns / count
    cosine = jnp.cos(angle_grid)
    sine = jnp.sin(angle_grid)
    upper = jnp.concatenate((cosine, sine), axis=1)
    lower = jnp.concatenate((-sine, cosine), axis=1)
    table = jnp.concatenate((upper, lower), axis=0).astype(jnp.bfloat16)
    return table.reshape(2, count, 2 * count).transpose(1, 0, 2).reshape(2 * count, 2 * count)


def chebyshev(cov_real, cov_imag, steer_real, steer_imag):
    high = lax.Precision.HIGH
    stations = cov_real.shape[1]
    loading = jnp.sum(jnp.diagonal(cov_real, axis1=1, axis2=2), axis=1) / stations
    row_mass = jnp.sum(jnp.sqrt(cov_real * cov_real + cov_imag * cov_imag), axis=2)
    bound = loading + jnp.max(row_mass, axis=1)
    center = ((bound + loading) / 2.0)[:, None, None]
    radius = ((bound - loading) / 2.0)[:, None, None]
    eye = jnp.eye(stations, dtype=jnp.float32)
    loaded = cov_real + loading[:, None, None] * eye
    block = jnp.concatenate(
        (
            jnp.concatenate((loaded, -cov_imag), axis=2),
            jnp.concatenate((cov_imag, loaded), axis=2),
        ),
        axis=1,
    )
    steer = jnp.concatenate((steer_real, steer_imag), axis=1)
    res = steer
    dirn = res / center
    sol = jnp.zeros_like(steer)
    rho = radius / center

    def body(_, carry):
        sol, res, dirn, rho = carry
        sol = sol + dirn
        img = jnp.einsum("cjk,ckb->cjb", block, dirn, precision=high)
        res = res - img
        rho_next = 1.0 / (2.0 * center / radius - rho)
        dirn = rho_next * rho * dirn + 2.0 * rho_next / radius * res
        return sol, res, dirn, rho_next

    sol, _, _, _ = lax.fori_loop(0, ITERS, body, (sol, res, dirn, rho), unroll=True)
    response = jnp.sum(steer * sol, axis=1, keepdims=True)
    weights = (sol / response).astype(jnp.bfloat16)
    return weights.reshape(weights.shape[0], 2, stations, weights.shape[2])


def exchange_phase(steer_phase, tm_size):
    own = lax.axis_index("tm")
    block = steer_phase.shape[0] // tm_size
    pieces = steer_phase.reshape(tm_size, block, *steer_phase.shape[1:])
    received = [lax.dynamic_index_in_dim(pieces, own, 0, keepdims=False)]
    for shift in range(1, tm_size):
        target = (own + shift) % tm_size
        outgoing = lax.dynamic_index_in_dim(pieces, target, 0, keepdims=False)
        perm = [(j, (j + shift) % tm_size) for j in range(tm_size)]
        received.append(lax.ppermute(outgoing, "tm", perm))
    stacked = jnp.stack(received, axis=0)
    order = (own - jnp.arange(tm_size)) % tm_size
    ordered = jnp.take(stacked, order, axis=0)
    return jnp.moveaxis(ordered, 0, 2).reshape(block, steer_phase.shape[1], -1)


def local(samples, station_gain, station_map, steer_phase):
    count = samples.shape[1]
    row_count = samples.shape[2]
    spec_count = samples.shape[3]
    chan_size = lax.axis_size("chan")
    tm_size = lax.axis_size("tm")
    channelized = jnp.dot(
        dft_table(count), samples.reshape(2 * count, -1), preferred_element_type=jnp.float32
    )
    channelized = channelized.reshape(count, 2, row_count, spec_count)
    spectra = (channelized * station_gain[None, None, :, None]).astype(jnp.bfloat16)
    split_channels = (count // chan_size) % tm_size == 0
    if split_channels:
        phase = exchange_phase(steer_phase, tm_size)
        spectra, phase = lax.optimization_barrier((spectra, phase))
    else:
        phase = steer_phase
    owned = lax.all_to_all(spectra, "chan", split_axis=0, concat_axis=2, tiled=True)
    chans = owned.shape[0]
    stations = owned.shape[2]
    stacked = owned.reshape(chans, 2 * stations, spec_count)
    spectra_total = spec_count * tm_size
    gram_sum = jnp.einsum("cat,cbt->cab", stacked, stacked, preferred_element_type=jnp.float32)
    part_real = gram_sum[:, :stations, :stations] + gram_sum[:, stations:, stations:]
    part_imag = gram_sum[:, stations:, :stations] - gram_sum[:, :stations, stations:]
    part = jnp.concatenate((part_real, part_imag), axis=1).astype(jnp.bfloat16)
    if split_channels:
        cov = lax.psum_scatter(part, "tm", scatter_dimension=0, tiled=True).astype(jnp.float32)
    else:
        cov = lax.psum(part, "tm").astype(jnp.float32)
    cov = cov / spectra_total
    phase_rows = jnp.take(phase, station_map, axis=1)
    weights = chebyshev(
        cov[:, :stations], cov[:, stations:], jnp.cos(phase_rows), jnp.sin(phase_rows)
    )
    if split_channels:
        weights = lax.all_gather(weights, "tm", axis=0, tiled=True)
    else:
        weights = lax.all_gather(weights, "tm", axis=3, tiled=True)
    weight_real = weights[:, 0]
    weight_imag = weights[:, 1]
    weight_cat = jnp.stack(
        (
            jnp.concatenate((weight_real, weight_imag), axis=1),
            jnp.concatenate((-weight_imag, weight_real), axis=1),
        ),
        axis=2,
    )
    formed = jnp.einsum("cat,cakb->ctkb", stacked, weight_cat, preferred_element_type=jnp.float32)
    return formed.astype(jnp.bfloat16)


def solution(mesh):
    in_specs = (
        P(None, None, ("groups", "chan"), "tm"),
        P(("groups", "chan")),
        P("groups"),
        P("chan", None, ("groups", "tm")),
    )
    out_specs = P("chan", "tm", None, "groups")
    return jax.shard_map(local, mesh=mesh, in_specs=in_specs, out_specs=out_specs, check_vma=False)
```

```python
import math

import jax
import jax.numpy as jnp
from jax import lax
from jax.sharding import PartitionSpec as P

ITERS = 8
TIME_PIECES = 2


def dft_table(count):
    index = jnp.arange(count, dtype=jnp.int32)
    turns = (index[:, None] * index[None, :] % count).astype(jnp.float32)
    angle_grid = 2.0 * math.pi * turns / count
    cosine = jnp.cos(angle_grid)
    sine = jnp.sin(angle_grid)
    upper = jnp.concatenate((cosine, sine), axis=1)
    lower = jnp.concatenate((-sine, cosine), axis=1)
    table = jnp.concatenate((upper, lower), axis=0).astype(jnp.bfloat16)
    return table.reshape(2, count, 2 * count).transpose(1, 0, 2).reshape(2 * count, 2 * count)


def chebyshev(cov_real, cov_imag, steer_real, steer_imag):
    high = lax.Precision.HIGH
    stations = cov_real.shape[1]
    loading = jnp.sum(jnp.diagonal(cov_real, axis1=1, axis2=2), axis=1) / stations
    row_mass = jnp.sum(jnp.sqrt(cov_real * cov_real + cov_imag * cov_imag), axis=2)
    bound = loading + jnp.max(row_mass, axis=1)
    center = ((bound + loading) / 2.0)[:, None, None]
    radius = ((bound - loading) / 2.0)[:, None, None]
    eye = jnp.eye(stations, dtype=jnp.float32)
    loaded = cov_real + loading[:, None, None] * eye
    block = jnp.concatenate(
        (
            jnp.concatenate((loaded, -cov_imag), axis=2),
            jnp.concatenate((cov_imag, loaded), axis=2),
        ),
        axis=1,
    )
    steer = jnp.concatenate((steer_real, steer_imag), axis=1)
    res = steer
    dirn = res / center
    sol = jnp.zeros_like(steer)
    rho = radius / center

    def body(_, carry):
        sol, res, dirn, rho = carry
        sol = sol + dirn
        img = jnp.einsum("cjk,ckb->cjb", block, dirn, precision=high)
        res = res - img
        rho_next = 1.0 / (2.0 * center / radius - rho)
        dirn = rho_next * rho * dirn + 2.0 * rho_next / radius * res
        return sol, res, dirn, rho_next

    sol, _, _, _ = lax.fori_loop(0, ITERS, body, (sol, res, dirn, rho), unroll=True)
    response = jnp.sum(steer * sol, axis=1, keepdims=True)
    weights = (sol / response).astype(jnp.bfloat16)
    return weights.reshape(weights.shape[0], 2, stations, weights.shape[2])


def exchange_phase(steer_phase, tm_size):
    own = lax.axis_index("tm")
    block = steer_phase.shape[0] // tm_size
    pieces = steer_phase.reshape(tm_size, block, *steer_phase.shape[1:])
    received = [lax.dynamic_index_in_dim(pieces, own, 0, keepdims=False)]
    for shift in range(1, tm_size):
        target = (own + shift) % tm_size
        outgoing = lax.dynamic_index_in_dim(pieces, target, 0, keepdims=False)
        perm = [(j, (j + shift) % tm_size) for j in range(tm_size)]
        received.append(lax.ppermute(outgoing, "tm", perm))
    stacked = jnp.stack(received, axis=0)
    order = (own - jnp.arange(tm_size)) % tm_size
    ordered = jnp.take(stacked, order, axis=0)
    return jnp.moveaxis(ordered, 0, 2).reshape(block, steer_phase.shape[1], -1)


def local(samples, station_gain, station_map, steer_phase):
    count = samples.shape[1]
    row_count = samples.shape[2]
    spec_count = samples.shape[3]
    chan_size = lax.axis_size("chan")
    tm_size = lax.axis_size("tm")
    split_channels = (count // chan_size) % tm_size == 0
    if split_channels:
        phase = exchange_phase(steer_phase, tm_size)
    else:
        phase = steer_phase
    table = dft_table(count)
    pieces = TIME_PIECES if spec_count % TIME_PIECES == 0 else 1
    width = spec_count // pieces
    owned_pieces = []
    for piece in range(pieces):
        chunk = samples[:, :, :, piece * width : (piece + 1) * width]
        channelized = jnp.dot(table, chunk.reshape(2 * count, -1), preferred_element_type=jnp.float32)
        channelized = channelized.reshape(count, 2, row_count, width)
        spectra = (channelized * station_gain[None, None, :, None]).astype(jnp.bfloat16)
        if split_channels and piece == 0:
            spectra, phase = lax.optimization_barrier((spectra, phase))
        owned_pieces.append(
            lax.all_to_all(spectra, "chan", split_axis=0, concat_axis=2, tiled=True)
        )
    owned = owned_pieces[0]
    chans = owned.shape[0]
    stations = owned.shape[2]
    stacked_pieces = [piece.reshape(chans, 2 * stations, width) for piece in owned_pieces]
    spectra_total = spec_count * tm_size
    gram_sum = None
    for stacked in stacked_pieces:
        gram = jnp.einsum("cat,cbt->cab", stacked, stacked, preferred_element_type=jnp.float32)
        gram_sum = gram if gram_sum is None else gram_sum + gram
    part_real = gram_sum[:, :stations, :stations] + gram_sum[:, stations:, stations:]
    part_imag = gram_sum[:, stations:, :stations] - gram_sum[:, :stations, stations:]
    part = jnp.concatenate((part_real, part_imag), axis=1).astype(jnp.bfloat16)
    if split_channels:
        cov = lax.psum_scatter(part, "tm", scatter_dimension=0, tiled=True).astype(jnp.float32)
    else:
        cov = lax.psum(part, "tm").astype(jnp.float32)
    cov = cov / spectra_total
    phase_rows = jnp.take(phase, station_map, axis=1)
    weights = chebyshev(
        cov[:, :stations], cov[:, stations:], jnp.cos(phase_rows), jnp.sin(phase_rows)
    )
    if split_channels:
        weights = lax.all_gather(weights, "tm", axis=0, tiled=True)
    else:
        weights = lax.all_gather(weights, "tm", axis=3, tiled=True)
    weight_real = weights[:, 0]
    weight_imag = weights[:, 1]
    weight_cat = jnp.stack(
        (
            jnp.concatenate((weight_real, weight_imag), axis=1),
            jnp.concatenate((-weight_imag, weight_real), axis=1),
        ),
        axis=2,
    )
    formed = [
        jnp.einsum("cat,cakb->ctkb", stacked, weight_cat, preferred_element_type=jnp.float32)
        for stacked in stacked_pieces
    ]
    return jnp.concatenate(formed, axis=1).astype(jnp.bfloat16)


def solution(mesh):
    in_specs = (
        P(None, None, ("groups", "chan"), "tm"),
        P(("groups", "chan")),
        P("groups"),
        P("chan", None, ("groups", "tm")),
    )
    out_specs = P("chan", "tm", None, "groups")
    return jax.shard_map(local, mesh=mesh, in_specs=in_specs, out_specs=out_specs, check_vma=False)
```

```python
import math

import jax
import jax.numpy as jnp
from jax import lax
from jax.sharding import PartitionSpec as P

ITERS = 8


def dft_table(count):
    index = jnp.arange(count, dtype=jnp.int32)
    turns = (index[:, None] * index[None, :] % count).astype(jnp.float32)
    angle_grid = 2.0 * math.pi * turns / count
    cosine = jnp.cos(angle_grid)
    sine = jnp.sin(angle_grid)
    upper = jnp.concatenate((cosine, sine), axis=1)
    lower = jnp.concatenate((-sine, cosine), axis=1)
    table = jnp.concatenate((upper, lower), axis=0).astype(jnp.bfloat16)
    return table.reshape(2, count, 2 * count).transpose(1, 0, 2).reshape(2 * count, 2 * count)


def chebyshev(cov_real, cov_imag, steer_real, steer_imag):
    high = lax.Precision.HIGH
    stations = cov_real.shape[1]
    loading = jnp.sum(jnp.diagonal(cov_real, axis1=1, axis2=2), axis=1) / stations
    row_mass = jnp.sum(jnp.sqrt(cov_real * cov_real + cov_imag * cov_imag), axis=2)
    bound = loading + jnp.max(row_mass, axis=1)
    center = ((bound + loading) / 2.0)[:, None, None]
    radius = ((bound - loading) / 2.0)[:, None, None]
    eye = jnp.eye(stations, dtype=jnp.float32)
    loaded = cov_real + loading[:, None, None] * eye
    block = jnp.concatenate(
        (
            jnp.concatenate((loaded, -cov_imag), axis=2),
            jnp.concatenate((cov_imag, loaded), axis=2),
        ),
        axis=1,
    )
    steer = jnp.concatenate((steer_real, steer_imag), axis=1)
    res = steer
    dirn = res / center
    sol = jnp.zeros_like(steer)
    rho = radius / center

    def body(_, carry):
        sol, res, dirn, rho = carry
        sol = sol + dirn
        img = jnp.einsum("cjk,ckb->cjb", block, dirn, precision=high)
        res = res - img
        rho_next = 1.0 / (2.0 * center / radius - rho)
        dirn = rho_next * rho * dirn + 2.0 * rho_next / radius * res
        return sol, res, dirn, rho_next

    sol, _, _, _ = lax.fori_loop(0, ITERS, body, (sol, res, dirn, rho), unroll=True)
    response = jnp.sum(steer * sol, axis=1, keepdims=True)
    weights = (sol / response).astype(jnp.bfloat16)
    return weights.reshape(weights.shape[0], 2, stations, weights.shape[2])


def exchange_phase(steer_phase, tm_size):
    own = lax.axis_index("tm")
    block = steer_phase.shape[0] // tm_size
    pieces = steer_phase.reshape(tm_size, block, *steer_phase.shape[1:])
    received = [lax.dynamic_index_in_dim(pieces, own, 0, keepdims=False)]
    for shift in range(1, tm_size):
        target = (own + shift) % tm_size
        outgoing = lax.dynamic_index_in_dim(pieces, target, 0, keepdims=False)
        perm = [(j, (j + shift) % tm_size) for j in range(tm_size)]
        received.append(lax.ppermute(outgoing, "tm", perm))
    stacked = jnp.stack(received, axis=0)
    order = (own - jnp.arange(tm_size)) % tm_size
    ordered = jnp.take(stacked, order, axis=0)
    return jnp.moveaxis(ordered, 0, 2).reshape(block, steer_phase.shape[1], -1)


def local(samples, station_gain, station_map, steer_phase):
    count = samples.shape[1]
    row_count = samples.shape[2]
    spec_count = samples.shape[3]
    chan_size = lax.axis_size("chan")
    tm_size = lax.axis_size("tm")
    channelized = jnp.dot(
        dft_table(count), samples.reshape(2 * count, -1), preferred_element_type=jnp.float32
    )
    channelized = channelized.reshape(count, 2, row_count, spec_count)
    spectra = (channelized * station_gain[None, None, :, None]).astype(jnp.bfloat16)
    split_channels = (count // chan_size) % tm_size == 0
    if split_channels:
        phase = exchange_phase(steer_phase, tm_size)
        spectra, phase = lax.optimization_barrier((spectra, phase))
    else:
        phase = steer_phase
    owned = lax.all_to_all(spectra, "chan", split_axis=0, concat_axis=2, tiled=True)
    chans = owned.shape[0]
    stations = owned.shape[2]
    stacked = owned.reshape(chans, 2 * stations, spec_count)
    spectra_total = spec_count * tm_size
    gram_sum = jnp.einsum("cat,cbt->cab", stacked, stacked, preferred_element_type=jnp.float32)
    part_real = gram_sum[:, :stations, :stations] + gram_sum[:, stations:, stations:]
    part_imag = gram_sum[:, stations:, :stations] - gram_sum[:, :stations, stations:]
    upper = jnp.arange(stations)[:, None] <= jnp.arange(stations)[None, :]
    if split_channels:
        part = jnp.where(upper, part_real, part_imag).astype(jnp.bfloat16)
    else:
        part = jnp.concatenate((part_real, part_imag), axis=1).astype(jnp.bfloat16)
    if split_channels:
        cov = lax.psum_scatter(part, "tm", scatter_dimension=0, tiled=True).astype(jnp.float32)
    else:
        cov = lax.psum(part, "tm").astype(jnp.float32)
    cov = cov / spectra_total
    if split_channels:
        cov_real = jnp.where(upper, cov, jnp.swapaxes(cov, 1, 2))
        below = jnp.where(upper, 0.0, cov)
        cov_imag = below - jnp.swapaxes(below, 1, 2)
        cov = jnp.concatenate((cov_real, cov_imag), axis=1)
    phase_rows = jnp.take(phase, station_map, axis=1)
    weights = chebyshev(
        cov[:, :stations], cov[:, stations:], jnp.cos(phase_rows), jnp.sin(phase_rows)
    )
    if split_channels:
        weights = lax.all_gather(weights, "tm", axis=0, tiled=True)
    else:
        weights = lax.all_gather(weights, "tm", axis=3, tiled=True)
    weight_real = weights[:, 0]
    weight_imag = weights[:, 1]
    weight_cat = jnp.stack(
        (
            jnp.concatenate((weight_real, weight_imag), axis=1),
            jnp.concatenate((-weight_imag, weight_real), axis=1),
        ),
        axis=2,
    )
    formed = jnp.einsum("cat,cakb->ctkb", stacked, weight_cat, preferred_element_type=jnp.float32)
    return formed.astype(jnp.bfloat16)


def solution(mesh):
    in_specs = (
        P(None, None, ("groups", "chan"), "tm"),
        P(("groups", "chan")),
        P("groups"),
        P("chan", None, ("groups", "tm")),
    )
    out_specs = P("chan", "tm", None, "groups")
    return jax.shard_map(local, mesh=mesh, in_specs=in_specs, out_specs=out_specs, check_vma=False)
```

```python
import math

import jax
import jax.numpy as jnp
from jax import lax
from jax.sharding import PartitionSpec as P

ITERS = 8


def dft_table(count):
    index = jnp.arange(count, dtype=jnp.int32)
    turns = (index[:, None] * index[None, :] % count).astype(jnp.float32)
    angle_grid = 2.0 * math.pi * turns / count
    cosine = jnp.cos(angle_grid)
    sine = jnp.sin(angle_grid)
    upper = jnp.concatenate((cosine, sine), axis=1)
    lower = jnp.concatenate((-sine, cosine), axis=1)
    table = jnp.concatenate((upper, lower), axis=0).astype(jnp.bfloat16)
    return table.reshape(2, count, 2 * count).transpose(1, 0, 2).reshape(2 * count, 2 * count)


def chebyshev(cov_real, cov_imag, steer_real, steer_imag):
    high = lax.Precision.HIGH
    stations = cov_real.shape[1]
    loading = jnp.sum(jnp.diagonal(cov_real, axis1=1, axis2=2), axis=1) / stations
    row_mass = jnp.sum(jnp.sqrt(cov_real * cov_real + cov_imag * cov_imag), axis=2)
    bound = loading + jnp.max(row_mass, axis=1)
    center = ((bound + loading) / 2.0)[:, None, None]
    radius = ((bound - loading) / 2.0)[:, None, None]
    eye = jnp.eye(stations, dtype=jnp.float32)
    loaded = cov_real + loading[:, None, None] * eye
    block = jnp.concatenate(
        (
            jnp.concatenate((loaded, -cov_imag), axis=2),
            jnp.concatenate((cov_imag, loaded), axis=2),
        ),
        axis=1,
    )
    steer = jnp.concatenate((steer_real, steer_imag), axis=1)
    res = steer
    dirn = res / center
    sol = jnp.zeros_like(steer)
    rho = radius / center

    def body(_, carry):
        sol, res, dirn, rho = carry
        sol = sol + dirn
        img = jnp.einsum("cjk,ckb->cjb", block, dirn, precision=high)
        res = res - img
        rho_next = 1.0 / (2.0 * center / radius - rho)
        dirn = rho_next * rho * dirn + 2.0 * rho_next / radius * res
        return sol, res, dirn, rho_next

    sol, _, _, _ = lax.fori_loop(0, ITERS, body, (sol, res, dirn, rho), unroll=True)
    response = jnp.sum(steer * sol, axis=1, keepdims=True)
    weights = (sol / response).astype(jnp.bfloat16)
    return weights.reshape(weights.shape[0], 2, stations, weights.shape[2])


def exchange_phase(steer_phase, tm_size):
    own = lax.axis_index("tm")
    block = steer_phase.shape[0] // tm_size
    pieces = steer_phase.reshape(tm_size, block, *steer_phase.shape[1:])
    received = [lax.dynamic_index_in_dim(pieces, own, 0, keepdims=False)]
    for shift in range(1, tm_size):
        target = (own + shift) % tm_size
        outgoing = lax.dynamic_index_in_dim(pieces, target, 0, keepdims=False)
        perm = [(j, (j + shift) % tm_size) for j in range(tm_size)]
        received.append(lax.ppermute(outgoing, "tm", perm))
    stacked = jnp.stack(received, axis=0)
    order = (own - jnp.arange(tm_size)) % tm_size
    ordered = jnp.take(stacked, order, axis=0)
    return jnp.moveaxis(ordered, 0, 2).reshape(block, steer_phase.shape[1], -1)


def local(samples, station_gain, station_map, steer_phase):
    count = samples.shape[1]
    row_count = samples.shape[2]
    spec_count = samples.shape[3]
    chan_size = lax.axis_size("chan")
    tm_size = lax.axis_size("tm")
    channelized = jnp.dot(
        dft_table(count), samples.reshape(2 * count, -1), preferred_element_type=jnp.float32
    )
    channelized = channelized.reshape(count, 2, row_count, spec_count)
    spectra = (channelized * station_gain[None, None, :, None]).astype(jnp.bfloat16)
    split_channels = (count // chan_size) % tm_size == 0
    if split_channels:
        phase = exchange_phase(steer_phase, tm_size)
        spectra, phase = lax.optimization_barrier((spectra, phase))
    else:
        phase = steer_phase
    owned = lax.all_to_all(spectra, "chan", split_axis=0, concat_axis=2, tiled=True)
    chans = owned.shape[0]
    stations = owned.shape[2]
    stacked = owned.reshape(chans, 2 * stations, spec_count)
    spectra_total = spec_count * tm_size
    gram_sum = jnp.einsum("cat,cbt->cab", stacked, stacked, preferred_element_type=jnp.float32)
    part_real = gram_sum[:, :stations, :stations] + gram_sum[:, stations:, stations:]
    part_imag = gram_sum[:, stations:, :stations] - gram_sum[:, :stations, stations:]
    upper = jnp.arange(stations)[:, None] <= jnp.arange(stations)[None, :]
    if split_channels:
        part = jnp.where(upper, part_real, part_imag).astype(jnp.bfloat16)
    else:
        part = jnp.concatenate((part_real, part_imag), axis=1).astype(jnp.bfloat16)
    if split_channels:
        cov = lax.psum_scatter(part, "tm", scatter_dimension=0, tiled=True).astype(jnp.float32)
    else:
        cov = lax.psum(part, "tm").astype(jnp.float32)
    cov = cov / spectra_total
    if split_channels:
        cov_real = jnp.where(upper, cov, jnp.swapaxes(cov, 1, 2))
        below = jnp.where(upper, 0.0, cov)
        cov_imag = below - jnp.swapaxes(below, 1, 2)
        cov = jnp.concatenate((cov_real, cov_imag), axis=1)
    phase_rows = jnp.take(phase, station_map, axis=1)
    steer_real = jnp.cos(phase_rows)
    steer_imag = jnp.sin(phase_rows)
    beam_count = steer_real.shape[2]
    halves = 2 if split_channels and beam_count % 256 == 0 else 1
    span = beam_count // halves
    formed = []
    for half in range(halves):
        beams = slice(half * span, (half + 1) * span)
        weights = chebyshev(
            cov[:, :stations], cov[:, stations:], steer_real[:, :, beams], steer_imag[:, :, beams]
        )
        if split_channels:
            weights = lax.all_gather(weights, "tm", axis=0, tiled=True)
        else:
            weights = lax.all_gather(weights, "tm", axis=3, tiled=True)
        weight_real = weights[:, 0]
        weight_imag = weights[:, 1]
        weight_cat = jnp.stack(
            (
                jnp.concatenate((weight_real, weight_imag), axis=1),
                jnp.concatenate((-weight_imag, weight_real), axis=1),
            ),
            axis=2,
        )
        formed.append(
            jnp.einsum("cat,cakb->ctkb", stacked, weight_cat, preferred_element_type=jnp.float32)
        )
    return jnp.concatenate(formed, axis=3).astype(jnp.bfloat16)


def solution(mesh):
    in_specs = (
        P(None, None, ("groups", "chan"), "tm"),
        P(("groups", "chan")),
        P("groups"),
        P("chan", None, ("groups", "tm")),
    )
    out_specs = P("chan", "tm", None, "groups")
    return jax.shard_map(local, mesh=mesh, in_specs=in_specs, out_specs=out_specs, check_vma=False)
```

```python
import math

import jax
import jax.numpy as jnp
from jax import lax
from jax.sharding import PartitionSpec as P

ITERS = 8


def dft_table(count):
    index = jnp.arange(count, dtype=jnp.int32)
    turns = (index[:, None] * index[None, :] % count).astype(jnp.float32)
    angle_grid = 2.0 * math.pi * turns / count
    cosine = jnp.cos(angle_grid)
    sine = jnp.sin(angle_grid)
    upper = jnp.concatenate((cosine, sine), axis=1)
    lower = jnp.concatenate((-sine, cosine), axis=1)
    table = jnp.concatenate((upper, lower), axis=0).astype(jnp.bfloat16)
    return table.reshape(2, count, 2 * count).transpose(1, 0, 2).reshape(2 * count, 2 * count)


def chebyshev(cov_real, cov_imag, steer_real, steer_imag):
    high = lax.Precision.HIGH
    stations = cov_real.shape[1]
    loading = jnp.sum(jnp.diagonal(cov_real, axis1=1, axis2=2), axis=1) / stations
    row_mass = jnp.sum(jnp.sqrt(cov_real * cov_real + cov_imag * cov_imag), axis=2)
    bound = loading + jnp.max(row_mass, axis=1)
    center = ((bound + loading) / 2.0)[:, None, None]
    radius = ((bound - loading) / 2.0)[:, None, None]
    eye = jnp.eye(stations, dtype=jnp.float32)
    loaded = cov_real + loading[:, None, None] * eye
    block = jnp.concatenate(
        (
            jnp.concatenate((loaded, -cov_imag), axis=2),
            jnp.concatenate((cov_imag, loaded), axis=2),
        ),
        axis=1,
    )
    steer = jnp.concatenate((steer_real, steer_imag), axis=1)
    res = steer
    dirn = res / center
    sol = jnp.zeros_like(steer)
    rho = radius / center

    def body(_, carry):
        sol, res, dirn, rho = carry
        sol = sol + dirn
        img = jnp.einsum("cjk,ckb->cjb", block, dirn, precision=high)
        res = res - img
        rho_next = 1.0 / (2.0 * center / radius - rho)
        dirn = rho_next * rho * dirn + 2.0 * rho_next / radius * res
        return sol, res, dirn, rho_next

    sol, _, _, _ = lax.fori_loop(0, ITERS, body, (sol, res, dirn, rho), unroll=True)
    response = jnp.sum(steer * sol, axis=1, keepdims=True)
    weights = (sol / response).astype(jnp.bfloat16)
    return weights.reshape(weights.shape[0], 2, stations, weights.shape[2])


def exchange_phase(steer_phase, tm_size):
    own = lax.axis_index("tm")
    block = steer_phase.shape[0] // tm_size
    pieces = steer_phase.reshape(tm_size, block, *steer_phase.shape[1:])
    received = [lax.dynamic_index_in_dim(pieces, own, 0, keepdims=False)]
    for shift in range(1, tm_size):
        target = (own + shift) % tm_size
        outgoing = lax.dynamic_index_in_dim(pieces, target, 0, keepdims=False)
        perm = [(j, (j + shift) % tm_size) for j in range(tm_size)]
        received.append(lax.ppermute(outgoing, "tm", perm))
    stacked = jnp.stack(received, axis=0)
    order = (own - jnp.arange(tm_size)) % tm_size
    ordered = jnp.take(stacked, order, axis=0)
    return jnp.moveaxis(ordered, 0, 2).reshape(block, steer_phase.shape[1], -1)


def local(samples, station_gain, station_map, steer_phase):
    count = samples.shape[1]
    row_count = samples.shape[2]
    spec_count = samples.shape[3]
    chan_size = lax.axis_size("chan")
    tm_size = lax.axis_size("tm")
    channelized = jnp.dot(
        dft_table(count), samples.reshape(2 * count, -1), preferred_element_type=jnp.float32
    )
    channelized = channelized.reshape(count, 2, row_count, spec_count)
    spectra = (channelized * station_gain[None, None, :, None]).astype(jnp.bfloat16)
    split_channels = (count // chan_size) % tm_size == 0
    if split_channels:
        phase = exchange_phase(steer_phase, tm_size)
        spectra, phase = lax.optimization_barrier((spectra, phase))
    else:
        phase = steer_phase
    owned = lax.all_to_all(spectra, "chan", split_axis=0, concat_axis=2, tiled=True)
    chans = owned.shape[0]
    stations = owned.shape[2]
    stacked = owned.reshape(chans, 2 * stations, spec_count)
    spectra_total = spec_count * tm_size
    gram_sum = jnp.einsum("cat,cbt->cab", stacked, stacked, preferred_element_type=jnp.float32)
    part_real = gram_sum[:, :stations, :stations] + gram_sum[:, stations:, stations:]
    part_imag = gram_sum[:, stations:, :stations] - gram_sum[:, :stations, stations:]
    upper = jnp.arange(stations)[:, None] <= jnp.arange(stations)[None, :]
    if split_channels:
        part = jnp.where(upper, part_real, part_imag).astype(jnp.bfloat16)
    else:
        part = jnp.concatenate((part_real, part_imag), axis=1).astype(jnp.bfloat16)
    if split_channels:
        cov = lax.psum_scatter(part, "tm", scatter_dimension=0, tiled=True).astype(jnp.float32)
    else:
        cov = lax.psum(part, "tm").astype(jnp.float32)
    cov = cov / spectra_total
    if split_channels:
        cov_real = jnp.where(upper, cov, jnp.swapaxes(cov, 1, 2))
        below = jnp.where(upper, 0.0, cov)
        cov_imag = below - jnp.swapaxes(below, 1, 2)
        cov = jnp.concatenate((cov_real, cov_imag), axis=1)
    phase_rows = jnp.take(phase, station_map, axis=1)
    steer_real = jnp.cos(phase_rows)
    steer_imag = jnp.sin(phase_rows)
    beam_count = steer_real.shape[2]
    halves = 2 if split_channels and beam_count % 256 == 0 else 1
    span = beam_count // halves
    gathered = []
    for half in range(halves):
        beams = slice(half * span, (half + 1) * span)
        weights = chebyshev(
            cov[:, :stations], cov[:, stations:], steer_real[:, :, beams], steer_imag[:, :, beams]
        )
        if split_channels:
            gathered.append(lax.all_gather(weights, "tm", axis=0, tiled=True))
        else:
            gathered.append(lax.all_gather(weights, "tm", axis=3, tiled=True))
    weights = jnp.concatenate(gathered, axis=3)
    weight_real = weights[:, 0]
    weight_imag = weights[:, 1]
    weight_cat = jnp.stack(
        (
            jnp.concatenate((weight_real, weight_imag), axis=1),
            jnp.concatenate((-weight_imag, weight_real), axis=1),
        ),
        axis=2,
    )
    formed = jnp.einsum("cat,cakb->ctkb", stacked, weight_cat, preferred_element_type=jnp.float32)
    return formed.astype(jnp.bfloat16)


def solution(mesh):
    in_specs = (
        P(None, None, ("groups", "chan"), "tm"),
        P(("groups", "chan")),
        P("groups"),
        P("chan", None, ("groups", "tm")),
    )
    out_specs = P("chan", "tm", None, "groups")
    return jax.shard_map(local, mesh=mesh, in_specs=in_specs, out_specs=out_specs, check_vma=False)
```

```python
import math

import jax
import jax.numpy as jnp
from jax import lax
from jax.sharding import PartitionSpec as P

ITERS = 8


def dft_table(count):
    index = jnp.arange(count, dtype=jnp.int32)
    turns = (index[:, None] * index[None, :] % count).astype(jnp.float32)
    angle_grid = 2.0 * math.pi * turns / count
    cosine = jnp.cos(angle_grid)
    sine = jnp.sin(angle_grid)
    upper = jnp.concatenate((cosine, sine), axis=1)
    lower = jnp.concatenate((-sine, cosine), axis=1)
    table = jnp.concatenate((upper, lower), axis=0).astype(jnp.bfloat16)
    return table.reshape(2, count, 2 * count).transpose(1, 0, 2).reshape(2 * count, 2 * count)


def chebyshev(cov_real, cov_imag, steer_real, steer_imag):
    high = lax.Precision.HIGH
    stations = cov_real.shape[1]
    eye = jnp.eye(stations, dtype=jnp.float32)
    loading = jnp.sum(jnp.where(eye > 0, cov_real, 0.0), axis=(1, 2)) / stations
    row_mass = jnp.sum(jnp.sqrt(cov_real * cov_real + cov_imag * cov_imag), axis=2)
    bound = loading + jnp.max(row_mass, axis=1)
    center = ((bound + loading) / 2.0)[:, None, None]
    radius = ((bound - loading) / 2.0)[:, None, None]
    loaded = cov_real + loading[:, None, None] * eye
    block = jnp.concatenate(
        (
            jnp.concatenate((loaded, -cov_imag), axis=2),
            jnp.concatenate((cov_imag, loaded), axis=2),
        ),
        axis=1,
    )
    steer = jnp.concatenate((steer_real, steer_imag), axis=1)
    res = steer
    dirn = res / center
    sol = jnp.zeros_like(steer)
    rho = radius / center

    def body(_, carry):
        sol, res, dirn, rho = carry
        sol = sol + dirn
        img = jnp.einsum("cjk,ckb->cjb", block, dirn, precision=high)
        res = res - img
        rho_next = 1.0 / (2.0 * center / radius - rho)
        dirn = rho_next * rho * dirn + 2.0 * rho_next / radius * res
        return sol, res, dirn, rho_next

    sol, _, _, _ = lax.fori_loop(0, ITERS, body, (sol, res, dirn, rho), unroll=True)
    response = jnp.sum(steer * sol, axis=1, keepdims=True)
    weights = (sol / response).astype(jnp.bfloat16)
    return weights.reshape(weights.shape[0], 2, stations, weights.shape[2])


def exchange_phase(steer_phase, tm_size):
    own = lax.axis_index("tm")
    block = steer_phase.shape[0] // tm_size
    pieces = steer_phase.reshape(tm_size, block, *steer_phase.shape[1:])
    received = [lax.dynamic_index_in_dim(pieces, own, 0, keepdims=False)]
    for shift in range(1, tm_size):
        target = (own + shift) % tm_size
        outgoing = lax.dynamic_index_in_dim(pieces, target, 0, keepdims=False)
        perm = [(j, (j + shift) % tm_size) for j in range(tm_size)]
        received.append(lax.ppermute(outgoing, "tm", perm))
    stacked = jnp.stack(received, axis=0)
    order = (own - jnp.arange(tm_size)) % tm_size
    ordered = jnp.take(stacked, order, axis=0)
    return jnp.moveaxis(ordered, 0, 2).reshape(block, steer_phase.shape[1], -1)


def local(samples, station_gain, station_map, steer_phase):
    count = samples.shape[1]
    row_count = samples.shape[2]
    spec_count = samples.shape[3]
    chan_size = lax.axis_size("chan")
    tm_size = lax.axis_size("tm")
    channelized = jnp.dot(
        dft_table(count), samples.reshape(2 * count, -1), preferred_element_type=jnp.float32
    )
    channelized = channelized.reshape(count, 2, row_count, spec_count)
    spectra = (channelized * station_gain[None, None, :, None]).astype(jnp.bfloat16)
    split_channels = (count // chan_size) % tm_size == 0
    if split_channels:
        phase = exchange_phase(steer_phase, tm_size)
        spectra, phase = lax.optimization_barrier((spectra, phase))
    else:
        phase = steer_phase
    owned = lax.all_to_all(spectra, "chan", split_axis=0, concat_axis=2, tiled=True)
    chans = owned.shape[0]
    stations = owned.shape[2]
    stacked = owned.reshape(chans, 2 * stations, spec_count)
    spectra_total = spec_count * tm_size
    gram_sum = jnp.einsum("cat,cbt->cab", stacked, stacked, preferred_element_type=jnp.float32)
    part_real = gram_sum[:, :stations, :stations] + gram_sum[:, stations:, stations:]
    part_imag = gram_sum[:, stations:, :stations] - gram_sum[:, :stations, stations:]
    upper = jnp.arange(stations)[:, None] <= jnp.arange(stations)[None, :]
    if split_channels:
        part = jnp.where(upper, part_real, part_imag).astype(jnp.bfloat16)
    else:
        part = jnp.concatenate((part_real, part_imag), axis=1).astype(jnp.bfloat16)
    if split_channels:
        cov = lax.psum_scatter(part, "tm", scatter_dimension=0, tiled=True).astype(jnp.float32)
    else:
        cov = lax.psum(part, "tm").astype(jnp.float32)
    cov = cov / spectra_total
    if split_channels:
        cov_real = jnp.where(upper, cov, jnp.swapaxes(cov, 1, 2))
        below = jnp.where(upper, 0.0, cov)
        cov_imag = below - jnp.swapaxes(below, 1, 2)
        cov = jnp.concatenate((cov_real, cov_imag), axis=1)
    phase_rows = jnp.take(phase, station_map, axis=1)
    weights = chebyshev(
        cov[:, :stations], cov[:, stations:], jnp.cos(phase_rows), jnp.sin(phase_rows)
    )
    if split_channels:
        weights = lax.all_gather(weights, "tm", axis=0, tiled=True)
    else:
        weights = lax.all_gather(weights, "tm", axis=3, tiled=True)
    weight_real = weights[:, 0]
    weight_imag = weights[:, 1]
    weight_cat = jnp.stack(
        (
            jnp.concatenate((weight_real, weight_imag), axis=1),
            jnp.concatenate((-weight_imag, weight_real), axis=1),
        ),
        axis=2,
    )
    formed = jnp.einsum("cat,cakb->ctkb", stacked, weight_cat, preferred_element_type=jnp.float32)
    return formed.astype(jnp.bfloat16)


def solution(mesh):
    in_specs = (
        P(None, None, ("groups", "chan"), "tm"),
        P(("groups", "chan")),
        P("groups"),
        P("chan", None, ("groups", "tm")),
    )
    out_specs = P("chan", "tm", None, "groups")
    return jax.shard_map(local, mesh=mesh, in_specs=in_specs, out_specs=out_specs, check_vma=False)
```

```python
import math

import jax
import jax.numpy as jnp
from jax import lax
from jax.sharding import PartitionSpec as P

ITERS = 8


def dft_table(count):
    index = jnp.arange(count, dtype=jnp.int32)
    turns = (index[:, None] * index[None, :] % count).astype(jnp.float32)
    angle_grid = 2.0 * math.pi * turns / count
    cosine = jnp.cos(angle_grid)
    sine = jnp.sin(angle_grid)
    upper = jnp.concatenate((cosine, sine), axis=1)
    lower = jnp.concatenate((-sine, cosine), axis=1)
    table = jnp.concatenate((upper, lower), axis=0).astype(jnp.bfloat16)
    return table.reshape(2, count, 2 * count).transpose(1, 0, 2).reshape(2 * count, 2 * count)


def chebyshev(cov_real, cov_imag, steer_real, steer_imag):
    high = lax.Precision.HIGH
    stations = cov_real.shape[1]
    eye = jnp.eye(stations, dtype=jnp.float32)
    loading = jnp.sum(jnp.where(eye > 0, cov_real, 0.0), axis=(1, 2)) / stations
    row_mass = jnp.sum(jnp.sqrt(cov_real * cov_real + cov_imag * cov_imag), axis=2)
    bound = loading + jnp.max(row_mass, axis=1)
    center = ((bound + loading) / 2.0)[:, None, None]
    radius = ((bound - loading) / 2.0)[:, None, None]
    loaded = cov_real + loading[:, None, None] * eye
    block = jnp.concatenate(
        (
            jnp.concatenate((loaded, -cov_imag), axis=2),
            jnp.concatenate((cov_imag, loaded), axis=2),
        ),
        axis=1,
    )
    steer = jnp.concatenate((steer_real, steer_imag), axis=1)
    res = steer
    dirn = res / center
    sol = jnp.zeros_like(steer)
    rho = radius / center

    def body(_, carry):
        sol, res, dirn, rho = carry
        sol = sol + dirn
        img = jnp.einsum("cjk,ckb->cjb", block, dirn, precision=high)
        res = res - img
        rho_next = 1.0 / (2.0 * center / radius - rho)
        dirn = rho_next * rho * dirn + 2.0 * rho_next / radius * res
        return sol, res, dirn, rho_next

    sol, _, _, _ = lax.fori_loop(0, ITERS, body, (sol, res, dirn, rho), unroll=True)
    response = jnp.sum(steer * sol, axis=1, keepdims=True)
    weights = (sol / response).astype(jnp.bfloat16)
    return weights.reshape(weights.shape[0], 2, stations, weights.shape[2])


def exchange_phase(steer_phase, tm_size):
    own = lax.axis_index("tm")
    block = steer_phase.shape[0] // tm_size
    pieces = steer_phase.reshape(tm_size, block, *steer_phase.shape[1:])
    received = [lax.dynamic_index_in_dim(pieces, own, 0, keepdims=False)]
    for shift in range(1, tm_size):
        target = (own + shift) % tm_size
        outgoing = lax.dynamic_index_in_dim(pieces, target, 0, keepdims=False)
        perm = [(j, (j + shift) % tm_size) for j in range(tm_size)]
        received.append(lax.ppermute(outgoing, "tm", perm))
    stacked = jnp.stack(received, axis=0)
    order = (own - jnp.arange(tm_size)) % tm_size
    ordered = jnp.take(stacked, order, axis=0)
    return jnp.moveaxis(ordered, 0, 2).reshape(block, steer_phase.shape[1], -1)


def local(samples, station_gain, station_map, steer_phase):
    count = samples.shape[1]
    row_count = samples.shape[2]
    spec_count = samples.shape[3]
    chan_size = lax.axis_size("chan")
    tm_size = lax.axis_size("tm")
    channelized = jnp.dot(
        dft_table(count), samples.reshape(2 * count, -1), preferred_element_type=jnp.float32
    )
    channelized = channelized.reshape(count, 2, row_count, spec_count)
    spectra = (channelized * station_gain[None, None, :, None]).astype(jnp.bfloat16)
    split_channels = (count // chan_size) % tm_size == 0
    if split_channels:
        phase = exchange_phase(steer_phase, tm_size)
        spectra, phase = lax.optimization_barrier((spectra, phase))
    else:
        phase = steer_phase
    owned = lax.all_to_all(spectra, "chan", split_axis=0, concat_axis=2, tiled=True)
    chans = owned.shape[0]
    stations = owned.shape[2]
    stacked = owned.reshape(chans, 2 * stations, spec_count)
    spectra_total = spec_count * tm_size
    turned = jnp.stack((owned[:, 1], -owned[:, 0]), axis=1)
    part_real = jnp.einsum("cpst,cput->csu", owned, owned, preferred_element_type=jnp.float32)
    part_imag = jnp.einsum("cpst,cput->csu", turned, owned, preferred_element_type=jnp.float32)
    upper = jnp.arange(stations)[:, None] <= jnp.arange(stations)[None, :]
    if split_channels:
        part = jnp.where(upper, part_real, part_imag).astype(jnp.bfloat16)
    else:
        part = jnp.concatenate((part_real, part_imag), axis=1).astype(jnp.bfloat16)
    if split_channels:
        cov = lax.psum_scatter(part, "tm", scatter_dimension=0, tiled=True).astype(jnp.float32)
    else:
        cov = lax.psum(part, "tm").astype(jnp.float32)
    cov = cov / spectra_total
    if split_channels:
        cov_real = jnp.where(upper, cov, jnp.swapaxes(cov, 1, 2))
        below = jnp.where(upper, 0.0, cov)
        cov_imag = below - jnp.swapaxes(below, 1, 2)
        cov = jnp.concatenate((cov_real, cov_imag), axis=1)
    phase_rows = jnp.take(phase, station_map, axis=1)
    weights = chebyshev(
        cov[:, :stations], cov[:, stations:], jnp.cos(phase_rows), jnp.sin(phase_rows)
    )
    if split_channels:
        weights = lax.all_gather(weights, "tm", axis=0, tiled=True)
    else:
        weights = lax.all_gather(weights, "tm", axis=3, tiled=True)
    weight_real = weights[:, 0]
    weight_imag = weights[:, 1]
    weight_cat = jnp.stack(
        (
            jnp.concatenate((weight_real, weight_imag), axis=1),
            jnp.concatenate((-weight_imag, weight_real), axis=1),
        ),
        axis=2,
    )
    formed = jnp.einsum("cat,cakb->ctkb", stacked, weight_cat, preferred_element_type=jnp.float32)
    return formed.astype(jnp.bfloat16)


def solution(mesh):
    in_specs = (
        P(None, None, ("groups", "chan"), "tm"),
        P(("groups", "chan")),
        P("groups"),
        P("chan", None, ("groups", "tm")),
    )
    out_specs = P("chan", "tm", None, "groups")
    return jax.shard_map(local, mesh=mesh, in_specs=in_specs, out_specs=out_specs, check_vma=False)
```

```python
import math

import jax
import jax.numpy as jnp
from jax import lax
from jax.experimental import pallas as pl
from jax.sharding import PartitionSpec as P

ITERS = 8


def dft_table(count):
    index = jnp.arange(count, dtype=jnp.int32)
    turns = (index[:, None] * index[None, :] % count).astype(jnp.float32)
    angle_grid = 2.0 * math.pi * turns / count
    cosine = jnp.cos(angle_grid)
    sine = jnp.sin(angle_grid)
    upper = jnp.concatenate((cosine, sine), axis=1)
    lower = jnp.concatenate((-sine, cosine), axis=1)
    table = jnp.concatenate((upper, lower), axis=0).astype(jnp.bfloat16)
    return table.reshape(2, count, 2 * count).transpose(1, 0, 2).reshape(2 * count, 2 * count)


def chebyshev(cov_real, cov_imag, steer_real, steer_imag):
    high = lax.Precision.HIGH
    stations = cov_real.shape[1]
    eye = jnp.eye(stations, dtype=jnp.float32)
    loading = jnp.sum(jnp.where(eye > 0, cov_real, 0.0), axis=(1, 2)) / stations
    row_mass = jnp.sum(jnp.sqrt(cov_real * cov_real + cov_imag * cov_imag), axis=2)
    bound = loading + jnp.max(row_mass, axis=1)
    center = ((bound + loading) / 2.0)[:, None, None]
    radius = ((bound - loading) / 2.0)[:, None, None]
    loaded = cov_real + loading[:, None, None] * eye
    block = jnp.concatenate(
        (
            jnp.concatenate((loaded, -cov_imag), axis=2),
            jnp.concatenate((cov_imag, loaded), axis=2),
        ),
        axis=1,
    )
    steer = jnp.concatenate((steer_real, steer_imag), axis=1)
    res = steer
    dirn = res / center
    sol = jnp.zeros_like(steer)
    rho = radius / center

    def body(_, carry):
        sol, res, dirn, rho = carry
        sol = sol + dirn
        img = jnp.einsum("cjk,ckb->cjb", block, dirn, precision=high)
        res = res - img
        rho_next = 1.0 / (2.0 * center / radius - rho)
        dirn = rho_next * rho * dirn + 2.0 * rho_next / radius * res
        return sol, res, dirn, rho_next

    sol, _, _, _ = lax.fori_loop(0, ITERS, body, (sol, res, dirn, rho), unroll=True)
    response = jnp.sum(steer * sol, axis=1, keepdims=True)
    weights = (sol / response).astype(jnp.bfloat16)
    return weights.reshape(weights.shape[0], 2, stations, weights.shape[2])


def exchange_phase(steer_phase, tm_size):
    own = lax.axis_index("tm")
    block = steer_phase.shape[0] // tm_size
    pieces = steer_phase.reshape(tm_size, block, *steer_phase.shape[1:])
    received = [lax.dynamic_index_in_dim(pieces, own, 0, keepdims=False)]
    for shift in range(1, tm_size):
        target = (own + shift) % tm_size
        outgoing = lax.dynamic_index_in_dim(pieces, target, 0, keepdims=False)
        perm = [(j, (j + shift) % tm_size) for j in range(tm_size)]
        received.append(lax.ppermute(outgoing, "tm", perm))
    stacked = jnp.stack(received, axis=0)
    order = (own - jnp.arange(tm_size)) % tm_size
    ordered = jnp.take(stacked, order, axis=0)
    return jnp.moveaxis(ordered, 0, 2).reshape(block, steer_phase.shape[1], -1)


def beam_kernel(x_ref, w_ref, o_ref):
    x = x_ref[...]
    for part in range(2):
        y = jnp.dot(w_ref[part], x, preferred_element_type=jnp.float32)
        o_ref[:, part, :] = y.T.astype(o_ref.dtype)


def beamform(stacked, weight_t):
    chans, rows, times = stacked.shape
    beams = weight_t.shape[2]
    block = 256 if times % 256 == 0 else times
    return pl.pallas_call(
        beam_kernel,
        grid=(chans, times // block),
        in_specs=[
            pl.BlockSpec((None, rows, block), lambda c, t: (c, 0, t)),
            pl.BlockSpec((None, 2, beams, rows), lambda c, t: (c, 0, 0, 0)),
        ],
        out_specs=pl.BlockSpec((None, block, 2, beams), lambda c, t: (c, t, 0, 0)),
        out_shape=jax.ShapeDtypeStruct((chans, times, 2, beams), jnp.bfloat16),
    )(stacked, weight_t)


def local(samples, station_gain, station_map, steer_phase):
    count = samples.shape[1]
    row_count = samples.shape[2]
    spec_count = samples.shape[3]
    chan_size = lax.axis_size("chan")
    tm_size = lax.axis_size("tm")
    channelized = jnp.dot(
        dft_table(count), samples.reshape(2 * count, -1), preferred_element_type=jnp.float32
    )
    channelized = channelized.reshape(count, 2, row_count, spec_count)
    spectra = (channelized * station_gain[None, None, :, None]).astype(jnp.bfloat16)
    split_channels = (count // chan_size) % tm_size == 0
    if split_channels:
        phase = exchange_phase(steer_phase, tm_size)
        spectra, phase = lax.optimization_barrier((spectra, phase))
    else:
        phase = steer_phase
    owned = lax.all_to_all(spectra, "chan", split_axis=0, concat_axis=2, tiled=True)
    chans = owned.shape[0]
    stations = owned.shape[2]
    stacked = owned.reshape(chans, 2 * stations, spec_count)
    spectra_total = spec_count * tm_size
    gram_sum = jnp.einsum("cat,cbt->cab", stacked, stacked, preferred_element_type=jnp.float32)
    part_real = gram_sum[:, :stations, :stations] + gram_sum[:, stations:, stations:]
    part_imag = gram_sum[:, stations:, :stations] - gram_sum[:, :stations, stations:]
    upper = jnp.arange(stations)[:, None] <= jnp.arange(stations)[None, :]
    if split_channels:
        part = jnp.where(upper, part_real, part_imag).astype(jnp.bfloat16)
    else:
        part = jnp.concatenate((part_real, part_imag), axis=1).astype(jnp.bfloat16)
    if split_channels:
        cov = lax.psum_scatter(part, "tm", scatter_dimension=0, tiled=True).astype(jnp.float32)
    else:
        cov = lax.psum(part, "tm").astype(jnp.float32)
    cov = cov / spectra_total
    if split_channels:
        cov_real = jnp.where(upper, cov, jnp.swapaxes(cov, 1, 2))
        below = jnp.where(upper, 0.0, cov)
        cov_imag = below - jnp.swapaxes(below, 1, 2)
        cov = jnp.concatenate((cov_real, cov_imag), axis=1)
    phase_rows = jnp.take(phase, station_map, axis=1)
    weights = chebyshev(
        cov[:, :stations], cov[:, stations:], jnp.cos(phase_rows), jnp.sin(phase_rows)
    )
    if split_channels:
        weights = lax.all_gather(weights, "tm", axis=0, tiled=True)
    else:
        weights = lax.all_gather(weights, "tm", axis=3, tiled=True)
    weight_real = weights[:, 0]
    weight_imag = weights[:, 1]
    real_t = jnp.swapaxes(weight_real, 1, 2)
    imag_t = jnp.swapaxes(weight_imag, 1, 2)
    weight_t = jnp.stack(
        (
            jnp.concatenate((real_t, imag_t), axis=2),
            jnp.concatenate((-imag_t, real_t), axis=2),
        ),
        axis=1,
    )
    return beamform(stacked, weight_t)


def solution(mesh):
    in_specs = (
        P(None, None, ("groups", "chan"), "tm"),
        P(("groups", "chan")),
        P("groups"),
        P("chan", None, ("groups", "tm")),
    )
    out_specs = P("chan", "tm", None, "groups")
    return jax.shard_map(local, mesh=mesh, in_specs=in_specs, out_specs=out_specs, check_vma=False)
```

```python
import math

import jax
import jax.numpy as jnp
from jax import lax
from jax.experimental import pallas as pl
from jax.sharding import PartitionSpec as P

ITERS = 8


def dft_table(count):
    index = jnp.arange(count, dtype=jnp.int32)
    turns = (index[:, None] * index[None, :] % count).astype(jnp.float32)
    angle_grid = 2.0 * math.pi * turns / count
    cosine = jnp.cos(angle_grid)
    sine = jnp.sin(angle_grid)
    upper = jnp.concatenate((cosine, sine), axis=1)
    lower = jnp.concatenate((-sine, cosine), axis=1)
    table = jnp.concatenate((upper, lower), axis=0).astype(jnp.bfloat16)
    return table.reshape(2, count, 2 * count).transpose(1, 0, 2).reshape(2 * count, 2 * count)


def chebyshev(cov_real, cov_imag, steer_real, steer_imag):
    high = lax.Precision.HIGH
    stations = cov_real.shape[1]
    eye = jnp.eye(stations, dtype=jnp.float32)
    loading = jnp.sum(jnp.where(eye > 0, cov_real, 0.0), axis=(1, 2)) / stations
    row_mass = jnp.sum(jnp.sqrt(cov_real * cov_real + cov_imag * cov_imag), axis=2)
    bound = loading + jnp.max(row_mass, axis=1)
    center = ((bound + loading) / 2.0)[:, None, None]
    radius = ((bound - loading) / 2.0)[:, None, None]
    loaded = cov_real + loading[:, None, None] * eye
    block = jnp.concatenate(
        (
            jnp.concatenate((loaded, -cov_imag), axis=2),
            jnp.concatenate((cov_imag, loaded), axis=2),
        ),
        axis=1,
    )
    steer = jnp.concatenate((steer_real, steer_imag), axis=1)
    res = steer
    dirn = res / center
    sol = jnp.zeros_like(steer)
    rho = radius / center

    def body(_, carry):
        sol, res, dirn, rho = carry
        sol = sol + dirn
        img = jnp.einsum("cjk,ckb->cjb", block, dirn, precision=high)
        res = res - img
        rho_next = 1.0 / (2.0 * center / radius - rho)
        dirn = rho_next * rho * dirn + 2.0 * rho_next / radius * res
        return sol, res, dirn, rho_next

    sol, _, _, _ = lax.fori_loop(0, ITERS, body, (sol, res, dirn, rho), unroll=True)
    response = jnp.sum(steer * sol, axis=1, keepdims=True)
    weights = (sol / response).astype(jnp.bfloat16)
    return weights.reshape(weights.shape[0], 2, stations, weights.shape[2])


def exchange_phase(steer_phase, tm_size):
    own = lax.axis_index("tm")
    block = steer_phase.shape[0] // tm_size
    pieces = steer_phase.reshape(tm_size, block, *steer_phase.shape[1:])
    received = [lax.dynamic_index_in_dim(pieces, own, 0, keepdims=False)]
    for shift in range(1, tm_size):
        target = (own + shift) % tm_size
        outgoing = lax.dynamic_index_in_dim(pieces, target, 0, keepdims=False)
        perm = [(j, (j + shift) % tm_size) for j in range(tm_size)]
        received.append(lax.ppermute(outgoing, "tm", perm))
    stacked = jnp.stack(received, axis=0)
    order = (own - jnp.arange(tm_size)) % tm_size
    ordered = jnp.take(stacked, order, axis=0)
    return jnp.moveaxis(ordered, 0, 2).reshape(block, steer_phase.shape[1], -1)


def beam_kernel(x_ref, w_ref, o_ref):
    xt = x_ref[...].T
    for part in range(2):
        y = jnp.dot(xt, w_ref[part], preferred_element_type=jnp.float32)
        o_ref[:, part, :] = y.astype(o_ref.dtype)


def beamform(stacked, weight_t):
    chans, rows, times = stacked.shape
    beams = weight_t.shape[3]
    block = 256 if times % 256 == 0 else times
    return pl.pallas_call(
        beam_kernel,
        grid=(chans, times // block),
        in_specs=[
            pl.BlockSpec((None, rows, block), lambda c, t: (c, 0, t)),
            pl.BlockSpec((None, 2, rows, beams), lambda c, t: (c, 0, 0, 0)),
        ],
        out_specs=pl.BlockSpec((None, block, 2, beams), lambda c, t: (c, t, 0, 0)),
        out_shape=jax.ShapeDtypeStruct((chans, times, 2, beams), jnp.bfloat16),
    )(stacked, weight_t)


def local(samples, station_gain, station_map, steer_phase):
    count = samples.shape[1]
    row_count = samples.shape[2]
    spec_count = samples.shape[3]
    chan_size = lax.axis_size("chan")
    tm_size = lax.axis_size("tm")
    channelized = jnp.dot(
        dft_table(count), samples.reshape(2 * count, -1), preferred_element_type=jnp.float32
    )
    channelized = channelized.reshape(count, 2, row_count, spec_count)
    spectra = (channelized * station_gain[None, None, :, None]).astype(jnp.bfloat16)
    split_channels = (count // chan_size) % tm_size == 0
    if split_channels:
        phase = exchange_phase(steer_phase, tm_size)
        spectra, phase = lax.optimization_barrier((spectra, phase))
    else:
        phase = steer_phase
    owned = lax.all_to_all(spectra, "chan", split_axis=0, concat_axis=2, tiled=True)
    chans = owned.shape[0]
    stations = owned.shape[2]
    stacked = owned.reshape(chans, 2 * stations, spec_count)
    spectra_total = spec_count * tm_size
    gram_sum = jnp.einsum("cat,cbt->cab", stacked, stacked, preferred_element_type=jnp.float32)
    part_real = gram_sum[:, :stations, :stations] + gram_sum[:, stations:, stations:]
    part_imag = gram_sum[:, stations:, :stations] - gram_sum[:, :stations, stations:]
    upper = jnp.arange(stations)[:, None] <= jnp.arange(stations)[None, :]
    if split_channels:
        part = jnp.where(upper, part_real, part_imag).astype(jnp.bfloat16)
    else:
        part = jnp.concatenate((part_real, part_imag), axis=1).astype(jnp.bfloat16)
    if split_channels:
        cov = lax.psum_scatter(part, "tm", scatter_dimension=0, tiled=True).astype(jnp.float32)
    else:
        cov = lax.psum(part, "tm").astype(jnp.float32)
    cov = cov / spectra_total
    if split_channels:
        cov_real = jnp.where(upper, cov, jnp.swapaxes(cov, 1, 2))
        below = jnp.where(upper, 0.0, cov)
        cov_imag = below - jnp.swapaxes(below, 1, 2)
        cov = jnp.concatenate((cov_real, cov_imag), axis=1)
    phase_rows = jnp.take(phase, station_map, axis=1)
    weights = chebyshev(
        cov[:, :stations], cov[:, stations:], jnp.cos(phase_rows), jnp.sin(phase_rows)
    )
    if split_channels:
        weights = lax.all_gather(weights, "tm", axis=0, tiled=True)
    else:
        weights = lax.all_gather(weights, "tm", axis=3, tiled=True)
    weight_real = weights[:, 0]
    weight_imag = weights[:, 1]
    weight_t = jnp.stack(
        (
            jnp.concatenate((weight_real, weight_imag), axis=1),
            jnp.concatenate((-weight_imag, weight_real), axis=1),
        ),
        axis=1,
    )
    return beamform(stacked, weight_t)


def solution(mesh):
    in_specs = (
        P(None, None, ("groups", "chan"), "tm"),
        P(("groups", "chan")),
        P("groups"),
        P("chan", None, ("groups", "tm")),
    )
    out_specs = P("chan", "tm", None, "groups")
    return jax.shard_map(local, mesh=mesh, in_specs=in_specs, out_specs=out_specs, check_vma=False)
```

```python
import math

import jax
import jax.numpy as jnp
from jax import lax
from jax.experimental import pallas as pl
from jax.sharding import PartitionSpec as P

ITERS = 8


def dft_table(count):
    index = jnp.arange(count, dtype=jnp.int32)
    turns = (index[:, None] * index[None, :] % count).astype(jnp.float32)
    angle_grid = 2.0 * math.pi * turns / count
    cosine = jnp.cos(angle_grid)
    sine = jnp.sin(angle_grid)
    upper = jnp.concatenate((cosine, sine), axis=1)
    lower = jnp.concatenate((-sine, cosine), axis=1)
    table = jnp.concatenate((upper, lower), axis=0).astype(jnp.bfloat16)
    return table.reshape(2, count, 2 * count).transpose(1, 0, 2).reshape(2 * count, 2 * count)


def chebyshev(cov_real, cov_imag, steer_real, steer_imag):
    high = lax.Precision.HIGH
    stations = cov_real.shape[1]
    eye = jnp.eye(stations, dtype=jnp.float32)
    loading = jnp.sum(jnp.where(eye > 0, cov_real, 0.0), axis=(1, 2)) / stations
    row_mass = jnp.sum(jnp.sqrt(cov_real * cov_real + cov_imag * cov_imag), axis=2)
    bound = loading + jnp.max(row_mass, axis=1)
    center = ((bound + loading) / 2.0)[:, None, None]
    radius = ((bound - loading) / 2.0)[:, None, None]
    loaded = cov_real + loading[:, None, None] * eye
    block = jnp.concatenate(
        (
            jnp.concatenate((loaded, -cov_imag), axis=2),
            jnp.concatenate((cov_imag, loaded), axis=2),
        ),
        axis=1,
    )
    steer = jnp.concatenate((steer_real, steer_imag), axis=1)
    res = steer
    dirn = res / center
    sol = jnp.zeros_like(steer)
    rho = radius / center

    def body(_, carry):
        sol, res, dirn, rho = carry
        sol = sol + dirn
        img = jnp.einsum("cjk,ckb->cjb", block, dirn, precision=high)
        res = res - img
        rho_next = 1.0 / (2.0 * center / radius - rho)
        dirn = rho_next * rho * dirn + 2.0 * rho_next / radius * res
        return sol, res, dirn, rho_next

    sol, _, _, _ = lax.fori_loop(0, ITERS, body, (sol, res, dirn, rho), unroll=True)
    response = jnp.sum(steer * sol, axis=1, keepdims=True)
    weights = (sol / response).astype(jnp.bfloat16)
    return weights.reshape(weights.shape[0], 2, stations, weights.shape[2])


def exchange_phase(steer_phase, tm_size):
    own = lax.axis_index("tm")
    block = steer_phase.shape[0] // tm_size
    pieces = steer_phase.reshape(tm_size, block, *steer_phase.shape[1:])
    received = [lax.dynamic_index_in_dim(pieces, own, 0, keepdims=False)]
    for shift in range(1, tm_size):
        target = (own + shift) % tm_size
        outgoing = lax.dynamic_index_in_dim(pieces, target, 0, keepdims=False)
        perm = [(j, (j + shift) % tm_size) for j in range(tm_size)]
        received.append(lax.ppermute(outgoing, "tm", perm))
    stacked = jnp.stack(received, axis=0)
    order = (own - jnp.arange(tm_size)) % tm_size
    ordered = jnp.take(stacked, order, axis=0)
    return jnp.moveaxis(ordered, 0, 2).reshape(block, steer_phase.shape[1], -1)


def beam_kernel(x_ref, w_ref, o_ref):
    stations = w_ref.shape[1]
    xt = x_ref[...].T
    x_real = xt[:, :stations]
    x_imag = xt[:, stations:]
    w_real = w_ref[0]
    w_imag = w_ref[1]
    f32 = jnp.float32
    beam_real = jnp.dot(x_real, w_real, preferred_element_type=f32) + jnp.dot(
        x_imag, w_imag, preferred_element_type=f32
    )
    beam_imag = jnp.dot(x_imag, w_real, preferred_element_type=f32) - jnp.dot(
        x_real, w_imag, preferred_element_type=f32
    )
    o_ref[:, 0, :] = beam_real.astype(o_ref.dtype)
    o_ref[:, 1, :] = beam_imag.astype(o_ref.dtype)


def beamform(stacked, weights):
    chans, rows, times = stacked.shape
    stations, beams = weights.shape[2], weights.shape[3]
    block = 256 if times % 256 == 0 else times
    return pl.pallas_call(
        beam_kernel,
        grid=(chans, times // block),
        in_specs=[
            pl.BlockSpec((None, rows, block), lambda c, t: (c, 0, t)),
            pl.BlockSpec((None, 2, stations, beams), lambda c, t: (c, 0, 0, 0)),
        ],
        out_specs=pl.BlockSpec((None, block, 2, beams), lambda c, t: (c, t, 0, 0)),
        out_shape=jax.ShapeDtypeStruct((chans, times, 2, beams), jnp.bfloat16),
    )(stacked, weights)


def local(samples, station_gain, station_map, steer_phase):
    count = samples.shape[1]
    row_count = samples.shape[2]
    spec_count = samples.shape[3]
    chan_size = lax.axis_size("chan")
    tm_size = lax.axis_size("tm")
    channelized = jnp.dot(
        dft_table(count), samples.reshape(2 * count, -1), preferred_element_type=jnp.float32
    )
    channelized = channelized.reshape(count, 2, row_count, spec_count)
    spectra = (channelized * station_gain[None, None, :, None]).astype(jnp.bfloat16)
    split_channels = (count // chan_size) % tm_size == 0
    if split_channels:
        phase = exchange_phase(steer_phase, tm_size)
        spectra, phase = lax.optimization_barrier((spectra, phase))
    else:
        phase = steer_phase
    owned = lax.all_to_all(spectra, "chan", split_axis=0, concat_axis=2, tiled=True)
    chans = owned.shape[0]
    stations = owned.shape[2]
    stacked = owned.reshape(chans, 2 * stations, spec_count)
    spectra_total = spec_count * tm_size
    gram_sum = jnp.einsum("cat,cbt->cab", stacked, stacked, preferred_element_type=jnp.float32)
    part_real = gram_sum[:, :stations, :stations] + gram_sum[:, stations:, stations:]
    part_imag = gram_sum[:, stations:, :stations] - gram_sum[:, :stations, stations:]
    upper = jnp.arange(stations)[:, None] <= jnp.arange(stations)[None, :]
    if split_channels:
        part = jnp.where(upper, part_real, part_imag).astype(jnp.bfloat16)
    else:
        part = jnp.concatenate((part_real, part_imag), axis=1).astype(jnp.bfloat16)
    if split_channels:
        cov = lax.psum_scatter(part, "tm", scatter_dimension=0, tiled=True).astype(jnp.float32)
    else:
        cov = lax.psum(part, "tm").astype(jnp.float32)
    cov = cov / spectra_total
    if split_channels:
        cov_real = jnp.where(upper, cov, jnp.swapaxes(cov, 1, 2))
        below = jnp.where(upper, 0.0, cov)
        cov_imag = below - jnp.swapaxes(below, 1, 2)
        cov = jnp.concatenate((cov_real, cov_imag), axis=1)
    phase_rows = jnp.take(phase, station_map, axis=1)
    weights = chebyshev(
        cov[:, :stations], cov[:, stations:], jnp.cos(phase_rows), jnp.sin(phase_rows)
    )
    if split_channels:
        weights = lax.all_gather(weights, "tm", axis=0, tiled=True)
    else:
        weights = lax.all_gather(weights, "tm", axis=3, tiled=True)
    return beamform(stacked, weights)


def solution(mesh):
    in_specs = (
        P(None, None, ("groups", "chan"), "tm"),
        P(("groups", "chan")),
        P("groups"),
        P("chan", None, ("groups", "tm")),
    )
    out_specs = P("chan", "tm", None, "groups")
    return jax.shard_map(local, mesh=mesh, in_specs=in_specs, out_specs=out_specs, check_vma=False)
```

```python
import math

import jax
import jax.numpy as jnp
from jax import lax
from jax.experimental import pallas as pl
from jax.experimental.pallas import tpu as pltpu
from jax.sharding import PartitionSpec as P

ITERS = 8


def dft_table(count):
    index = jnp.arange(count, dtype=jnp.int32)
    turns = (index[:, None] * index[None, :] % count).astype(jnp.float32)
    angle_grid = 2.0 * math.pi * turns / count
    cosine = jnp.cos(angle_grid)
    sine = jnp.sin(angle_grid)
    upper = jnp.concatenate((cosine, sine), axis=1)
    lower = jnp.concatenate((-sine, cosine), axis=1)
    table = jnp.concatenate((upper, lower), axis=0).astype(jnp.bfloat16)
    return table.reshape(2, count, 2 * count).transpose(1, 0, 2).reshape(2 * count, 2 * count)


def chebyshev(cov_real, cov_imag, steer_real, steer_imag):
    high = lax.Precision.HIGH
    stations = cov_real.shape[1]
    eye = jnp.eye(stations, dtype=jnp.float32)
    loading = jnp.sum(jnp.where(eye > 0, cov_real, 0.0), axis=(1, 2)) / stations
    row_mass = jnp.sum(jnp.sqrt(cov_real * cov_real + cov_imag * cov_imag), axis=2)
    bound = loading + jnp.max(row_mass, axis=1)
    center = ((bound + loading) / 2.0)[:, None, None]
    radius = ((bound - loading) / 2.0)[:, None, None]
    loaded = cov_real + loading[:, None, None] * eye
    block = jnp.concatenate(
        (
            jnp.concatenate((loaded, -cov_imag), axis=2),
            jnp.concatenate((cov_imag, loaded), axis=2),
        ),
        axis=1,
    )
    steer = jnp.concatenate((steer_real, steer_imag), axis=1)
    res = steer
    dirn = res / center
    sol = jnp.zeros_like(steer)
    rho = radius / center

    def body(_, carry):
        sol, res, dirn, rho = carry
        sol = sol + dirn
        img = jnp.einsum("cjk,ckb->cjb", block, dirn, precision=high)
        res = res - img
        rho_next = 1.0 / (2.0 * center / radius - rho)
        dirn = rho_next * rho * dirn + 2.0 * rho_next / radius * res
        return sol, res, dirn, rho_next

    sol, _, _, _ = lax.fori_loop(0, ITERS, body, (sol, res, dirn, rho), unroll=True)
    response = jnp.sum(steer * sol, axis=1, keepdims=True)
    weights = (sol / response).astype(jnp.bfloat16)
    return weights.reshape(weights.shape[0], 2, stations, weights.shape[2])


def exchange_phase(steer_phase, tm_size):
    own = lax.axis_index("tm")
    block = steer_phase.shape[0] // tm_size
    pieces = steer_phase.reshape(tm_size, block, *steer_phase.shape[1:])
    received = [lax.dynamic_index_in_dim(pieces, own, 0, keepdims=False)]
    for shift in range(1, tm_size):
        target = (own + shift) % tm_size
        outgoing = lax.dynamic_index_in_dim(pieces, target, 0, keepdims=False)
        perm = [(j, (j + shift) % tm_size) for j in range(tm_size)]
        received.append(lax.ppermute(outgoing, "tm", perm))
    stacked = jnp.stack(received, axis=0)
    order = (own - jnp.arange(tm_size)) % tm_size
    ordered = jnp.take(stacked, order, axis=0)
    return jnp.moveaxis(ordered, 0, 2).reshape(block, steer_phase.shape[1], -1)


def dft_kernel(t_ref, g_ref, x_ref, o_ref):
    base = pl.program_id(0) * x_ref.shape[1]
    table = t_ref[...]
    for row in range(x_ref.shape[1]):
        y = jnp.dot(table, x_ref[:, row, :], preferred_element_type=jnp.float32)
        o_ref[:, row, :] = (y * g_ref[base + row]).astype(o_ref.dtype)


def channelize(table, samples, station_gain):
    parts, count, rows, times = samples.shape
    flat = samples.reshape(parts * count, rows, times)
    block = 16 if rows % 16 == 0 else rows
    out = pl.pallas_call(
        dft_kernel,
        grid=(rows // block,),
        in_specs=[
            pl.BlockSpec((parts * count, parts * count), lambda i: (0, 0)),
            pl.BlockSpec(memory_space=pltpu.SMEM),
            pl.BlockSpec((parts * count, block, times), lambda i: (0, i, 0)),
        ],
        out_specs=pl.BlockSpec((parts * count, block, times), lambda i: (0, i, 0)),
        out_shape=jax.ShapeDtypeStruct((parts * count, rows, times), jnp.bfloat16),
    )(table, station_gain, flat)
    return out.reshape(count, parts, rows, times)


def beam_kernel(x_ref, w_ref, o_ref):
    stations = w_ref.shape[1]
    xt = x_ref[...].T
    x_real = xt[:, :stations]
    x_imag = xt[:, stations:]
    w_real = w_ref[0]
    w_imag = w_ref[1]
    f32 = jnp.float32
    beam_real = jnp.dot(x_real, w_real, preferred_element_type=f32) + jnp.dot(
        x_imag, w_imag, preferred_element_type=f32
    )
    beam_imag = jnp.dot(x_imag, w_real, preferred_element_type=f32) - jnp.dot(
        x_real, w_imag, preferred_element_type=f32
    )
    o_ref[:, 0, :] = beam_real.astype(o_ref.dtype)
    o_ref[:, 1, :] = beam_imag.astype(o_ref.dtype)


def beamform(stacked, weights):
    chans, rows, times = stacked.shape
    stations, beams = weights.shape[2], weights.shape[3]
    block = 256 if times % 256 == 0 else times
    return pl.pallas_call(
        beam_kernel,
        grid=(chans, times // block),
        in_specs=[
            pl.BlockSpec((None, rows, block), lambda c, t: (c, 0, t)),
            pl.BlockSpec((None, 2, stations, beams), lambda c, t: (c, 0, 0, 0)),
        ],
        out_specs=pl.BlockSpec((None, block, 2, beams), lambda c, t: (c, t, 0, 0)),
        out_shape=jax.ShapeDtypeStruct((chans, times, 2, beams), jnp.bfloat16),
    )(stacked, weights)


def local(samples, station_gain, station_map, steer_phase):
    count = samples.shape[1]
    row_count = samples.shape[2]
    spec_count = samples.shape[3]
    chan_size = lax.axis_size("chan")
    tm_size = lax.axis_size("tm")
    spectra = channelize(dft_table(count), samples, station_gain)
    split_channels = (count // chan_size) % tm_size == 0
    if split_channels:
        phase = exchange_phase(steer_phase, tm_size)
        spectra, phase = lax.optimization_barrier((spectra, phase))
    else:
        phase = steer_phase
    owned = lax.all_to_all(spectra, "chan", split_axis=0, concat_axis=2, tiled=True)
    chans = owned.shape[0]
    stations = owned.shape[2]
    stacked = owned.reshape(chans, 2 * stations, spec_count)
    spectra_total = spec_count * tm_size
    gram_sum = jnp.einsum("cat,cbt->cab", stacked, stacked, preferred_element_type=jnp.float32)
    part_real = gram_sum[:, :stations, :stations] + gram_sum[:, stations:, stations:]
    part_imag = gram_sum[:, stations:, :stations] - gram_sum[:, :stations, stations:]
    upper = jnp.arange(stations)[:, None] <= jnp.arange(stations)[None, :]
    if split_channels:
        part = jnp.where(upper, part_real, part_imag).astype(jnp.bfloat16)
    else:
        part = jnp.concatenate((part_real, part_imag), axis=1).astype(jnp.bfloat16)
    if split_channels:
        cov = lax.psum_scatter(part, "tm", scatter_dimension=0, tiled=True).astype(jnp.float32)
    else:
        cov = lax.psum(part, "tm").astype(jnp.float32)
    cov = cov / spectra_total
    if split_channels:
        cov_real = jnp.where(upper, cov, jnp.swapaxes(cov, 1, 2))
        below = jnp.where(upper, 0.0, cov)
        cov_imag = below - jnp.swapaxes(below, 1, 2)
        cov = jnp.concatenate((cov_real, cov_imag), axis=1)
    phase_rows = jnp.take(phase, station_map, axis=1)
    weights = chebyshev(
        cov[:, :stations], cov[:, stations:], jnp.cos(phase_rows), jnp.sin(phase_rows)
    )
    if split_channels:
        weights = lax.all_gather(weights, "tm", axis=0, tiled=True)
    else:
        weights = lax.all_gather(weights, "tm", axis=3, tiled=True)
    return beamform(stacked, weights)


def solution(mesh):
    in_specs = (
        P(None, None, ("groups", "chan"), "tm"),
        P(("groups", "chan")),
        P("groups"),
        P("chan", None, ("groups", "tm")),
    )
    out_specs = P("chan", "tm", None, "groups")
    return jax.shard_map(local, mesh=mesh, in_specs=in_specs, out_specs=out_specs, check_vma=False)
```

```python
import math

import jax
import jax.numpy as jnp
from jax import lax
from jax.experimental import pallas as pl
from jax.experimental.pallas import tpu as pltpu
from jax.sharding import PartitionSpec as P

ITERS = 8


def dft_table(count):
    index = jnp.arange(count, dtype=jnp.int32)
    turns = (index[:, None] * index[None, :] % count).astype(jnp.float32)
    angle_grid = 2.0 * math.pi * turns / count
    cosine = jnp.cos(angle_grid)
    sine = jnp.sin(angle_grid)
    upper = jnp.concatenate((cosine, sine), axis=1)
    lower = jnp.concatenate((-sine, cosine), axis=1)
    table = jnp.concatenate((upper, lower), axis=0).astype(jnp.bfloat16)
    return table.reshape(2, count, 2 * count).transpose(1, 0, 2).reshape(2 * count, 2 * count)


def chebyshev(cov_real, cov_imag, steer_real, steer_imag):
    high = lax.Precision.HIGH
    stations = cov_real.shape[1]
    eye = jnp.eye(stations, dtype=jnp.float32)
    loading = jnp.sum(jnp.where(eye > 0, cov_real, 0.0), axis=(1, 2)) / stations
    row_mass = jnp.sum(jnp.sqrt(cov_real * cov_real + cov_imag * cov_imag), axis=2)
    bound = loading + jnp.max(row_mass, axis=1)
    center = ((bound + loading) / 2.0)[:, None, None]
    radius = ((bound - loading) / 2.0)[:, None, None]
    loaded = cov_real + loading[:, None, None] * eye
    block = jnp.concatenate(
        (
            jnp.concatenate((loaded, -cov_imag), axis=2),
            jnp.concatenate((cov_imag, loaded), axis=2),
        ),
        axis=1,
    )
    steer = jnp.concatenate((steer_real, steer_imag), axis=1)
    res = steer
    dirn = res / center
    sol = jnp.zeros_like(steer)
    rho = radius / center

    def body(_, carry):
        sol, res, dirn, rho = carry
        sol = sol + dirn
        img = jnp.einsum("cjk,ckb->cjb", block, dirn, precision=high)
        res = res - img
        rho_next = 1.0 / (2.0 * center / radius - rho)
        dirn = rho_next * rho * dirn + 2.0 * rho_next / radius * res
        return sol, res, dirn, rho_next

    sol, _, _, _ = lax.fori_loop(0, ITERS, body, (sol, res, dirn, rho), unroll=True)
    response = jnp.sum(steer * sol, axis=1, keepdims=True)
    weights = (sol / response).astype(jnp.bfloat16)
    return weights.reshape(weights.shape[0], 2, stations, weights.shape[2])


def exchange_phase(steer_phase, tm_size):
    own = lax.axis_index("tm")
    block = steer_phase.shape[0] // tm_size
    pieces = steer_phase.reshape(tm_size, block, *steer_phase.shape[1:])
    received = [lax.dynamic_index_in_dim(pieces, own, 0, keepdims=False)]
    for shift in range(1, tm_size):
        target = (own + shift) % tm_size
        outgoing = lax.dynamic_index_in_dim(pieces, target, 0, keepdims=False)
        perm = [(j, (j + shift) % tm_size) for j in range(tm_size)]
        received.append(lax.ppermute(outgoing, "tm", perm))
    stacked = jnp.stack(received, axis=0)
    order = (own - jnp.arange(tm_size)) % tm_size
    ordered = jnp.take(stacked, order, axis=0)
    return jnp.moveaxis(ordered, 0, 2).reshape(block, steer_phase.shape[1], -1)


def dft_kernel(t_ref, g_ref, x_ref, o_ref):
    base = pl.program_id(0) * x_ref.shape[1]
    table = t_ref[...]
    for row in range(x_ref.shape[1]):
        y = jnp.dot(table, x_ref[:, row, :], preferred_element_type=jnp.float32)
        o_ref[:, row, :] = (y * g_ref[base + row]).astype(o_ref.dtype)


def channelize(table, samples, station_gain):
    parts, count, rows, times = samples.shape
    flat = samples.reshape(parts * count, rows, times)
    block = 16 if rows % 16 == 0 else rows
    out = pl.pallas_call(
        dft_kernel,
        grid=(rows // block,),
        in_specs=[
            pl.BlockSpec((parts * count, parts * count), lambda i: (0, 0)),
            pl.BlockSpec(memory_space=pltpu.SMEM),
            pl.BlockSpec((parts * count, block, times), lambda i: (0, i, 0)),
        ],
        out_specs=pl.BlockSpec((parts * count, block, times), lambda i: (0, i, 0)),
        out_shape=jax.ShapeDtypeStruct((parts * count, rows, times), jnp.bfloat16),
    )(table, station_gain, flat)
    return out.reshape(count, parts, rows, times)


def beam_kernel(x_ref, w_ref, o_ref):
    stations = w_ref.shape[1]
    xt = x_ref[...].T
    x_real = xt[:, :stations]
    x_imag = xt[:, stations:]
    w_real = w_ref[0]
    w_imag = w_ref[1]
    f32 = jnp.float32
    beam_real = jnp.dot(x_real, w_real, preferred_element_type=f32) + jnp.dot(
        x_imag, w_imag, preferred_element_type=f32
    )
    beam_imag = jnp.dot(x_imag, w_real, preferred_element_type=f32) - jnp.dot(
        x_real, w_imag, preferred_element_type=f32
    )
    o_ref[:, 0, :] = beam_real.astype(o_ref.dtype)
    o_ref[:, 1, :] = beam_imag.astype(o_ref.dtype)


def beamform(stacked, weights):
    chans, rows, times = stacked.shape
    stations, beams = weights.shape[2], weights.shape[3]
    block = 512 if times % 512 == 0 else times
    return pl.pallas_call(
        beam_kernel,
        grid=(chans, times // block),
        in_specs=[
            pl.BlockSpec((None, rows, block), lambda c, t: (c, 0, t)),
            pl.BlockSpec((None, 2, stations, beams), lambda c, t: (c, 0, 0, 0)),
        ],
        out_specs=pl.BlockSpec((None, block, 2, beams), lambda c, t: (c, t, 0, 0)),
        out_shape=jax.ShapeDtypeStruct((chans, times, 2, beams), jnp.bfloat16),
    )(stacked, weights)


def local(samples, station_gain, station_map, steer_phase):
    count = samples.shape[1]
    row_count = samples.shape[2]
    spec_count = samples.shape[3]
    chan_size = lax.axis_size("chan")
    tm_size = lax.axis_size("tm")
    spectra = channelize(dft_table(count), samples, station_gain)
    split_channels = (count // chan_size) % tm_size == 0
    if split_channels:
        phase = exchange_phase(steer_phase, tm_size)
        spectra, phase = lax.optimization_barrier((spectra, phase))
    else:
        phase = steer_phase
    owned = lax.all_to_all(spectra, "chan", split_axis=0, concat_axis=2, tiled=True)
    chans = owned.shape[0]
    stations = owned.shape[2]
    stacked = owned.reshape(chans, 2 * stations, spec_count)
    spectra_total = spec_count * tm_size
    gram_sum = jnp.einsum("cat,cbt->cab", stacked, stacked, preferred_element_type=jnp.float32)
    part_real = gram_sum[:, :stations, :stations] + gram_sum[:, stations:, stations:]
    part_imag = gram_sum[:, stations:, :stations] - gram_sum[:, :stations, stations:]
    upper = jnp.arange(stations)[:, None] <= jnp.arange(stations)[None, :]
    if split_channels:
        part = jnp.where(upper, part_real, part_imag).astype(jnp.bfloat16)
    else:
        part = jnp.concatenate((part_real, part_imag), axis=1).astype(jnp.bfloat16)
    if split_channels:
        cov = lax.psum_scatter(part, "tm", scatter_dimension=0, tiled=True).astype(jnp.float32)
    else:
        cov = lax.psum(part, "tm").astype(jnp.float32)
    cov = cov / spectra_total
    if split_channels:
        cov_real = jnp.where(upper, cov, jnp.swapaxes(cov, 1, 2))
        below = jnp.where(upper, 0.0, cov)
        cov_imag = below - jnp.swapaxes(below, 1, 2)
        cov = jnp.concatenate((cov_real, cov_imag), axis=1)
    phase_rows = jnp.take(phase, station_map, axis=1)
    weights = chebyshev(
        cov[:, :stations], cov[:, stations:], jnp.cos(phase_rows), jnp.sin(phase_rows)
    )
    if split_channels:
        weights = lax.all_gather(weights, "tm", axis=0, tiled=True)
    else:
        weights = lax.all_gather(weights, "tm", axis=3, tiled=True)
    return beamform(stacked, weights)


def solution(mesh):
    in_specs = (
        P(None, None, ("groups", "chan"), "tm"),
        P(("groups", "chan")),
        P("groups"),
        P("chan", None, ("groups", "tm")),
    )
    out_specs = P("chan", "tm", None, "groups")
    return jax.shard_map(local, mesh=mesh, in_specs=in_specs, out_specs=out_specs, check_vma=False)
```

```python
import math

import jax
import jax.numpy as jnp
from jax import lax
from jax.experimental import pallas as pl
from jax.experimental.pallas import tpu as pltpu
from jax.sharding import PartitionSpec as P

ITERS = 8


def dft_table(count):
    index = jnp.arange(count, dtype=jnp.int32)
    turns = (index[:, None] * index[None, :] % count).astype(jnp.float32)
    angle_grid = 2.0 * math.pi * turns / count
    cosine = jnp.cos(angle_grid)
    sine = jnp.sin(angle_grid)
    upper = jnp.concatenate((cosine, sine), axis=1)
    lower = jnp.concatenate((-sine, cosine), axis=1)
    table = jnp.concatenate((upper, lower), axis=0).astype(jnp.bfloat16)
    return table.reshape(2, count, 2 * count).transpose(1, 0, 2).reshape(2 * count, 2 * count)


def chebyshev(cov_real, cov_imag, steer_real, steer_imag):
    high = lax.Precision.HIGH
    stations = cov_real.shape[1]
    eye = jnp.eye(stations, dtype=jnp.float32)
    loading = jnp.sum(jnp.where(eye > 0, cov_real, 0.0), axis=(1, 2)) / stations
    row_mass = jnp.sum(jnp.sqrt(cov_real * cov_real + cov_imag * cov_imag), axis=2)
    bound = loading + jnp.max(row_mass, axis=1)
    center = ((bound + loading) / 2.0)[:, None, None]
    radius = ((bound - loading) / 2.0)[:, None, None]
    loaded = cov_real + loading[:, None, None] * eye
    block = jnp.concatenate(
        (
            jnp.concatenate((loaded, -cov_imag), axis=2),
            jnp.concatenate((cov_imag, loaded), axis=2),
        ),
        axis=1,
    )
    steer = jnp.concatenate((steer_real, steer_imag), axis=1)
    res = steer
    dirn = res / center
    sol = jnp.zeros_like(steer)
    rho = radius / center

    def body(_, carry):
        sol, res, dirn, rho = carry
        sol = sol + dirn
        img = jnp.einsum("cjk,ckb->cjb", block, dirn, precision=high)
        res = res - img
        rho_next = 1.0 / (2.0 * center / radius - rho)
        dirn = rho_next * rho * dirn + 2.0 * rho_next / radius * res
        return sol, res, dirn, rho_next

    sol, _, _, _ = lax.fori_loop(0, ITERS, body, (sol, res, dirn, rho), unroll=True)
    response = jnp.sum(steer * sol, axis=1, keepdims=True)
    weights = (sol / response).astype(jnp.bfloat16)
    return weights.reshape(weights.shape[0], 2, stations, weights.shape[2])


def exchange_phase(steer_phase, tm_size):
    own = lax.axis_index("tm")
    block = steer_phase.shape[0] // tm_size
    pieces = steer_phase.reshape(tm_size, block, *steer_phase.shape[1:])
    received = [lax.dynamic_index_in_dim(pieces, own, 0, keepdims=False)]
    for shift in range(1, tm_size):
        target = (own + shift) % tm_size
        outgoing = lax.dynamic_index_in_dim(pieces, target, 0, keepdims=False)
        perm = [(j, (j + shift) % tm_size) for j in range(tm_size)]
        received.append(lax.ppermute(outgoing, "tm", perm))
    stacked = jnp.stack(received, axis=0)
    order = (own - jnp.arange(tm_size)) % tm_size
    ordered = jnp.take(stacked, order, axis=0)
    return jnp.moveaxis(ordered, 0, 2).reshape(block, steer_phase.shape[1], -1)


def dft_kernel(t_ref, g_ref, x_ref, o_ref):
    base = pl.program_id(0) * x_ref.shape[1]
    table = t_ref[...]
    for row in range(x_ref.shape[1]):
        y = jnp.dot(table, x_ref[:, row, :], preferred_element_type=jnp.float32)
        o_ref[:, row, :] = (y * g_ref[base + row]).astype(o_ref.dtype)


def channelize(table, samples, station_gain):
    parts, count, rows, times = samples.shape
    flat = samples.reshape(parts * count, rows, times)
    block = 16 if rows % 16 == 0 else rows
    out = pl.pallas_call(
        dft_kernel,
        grid=(rows // block,),
        in_specs=[
            pl.BlockSpec((parts * count, parts * count), lambda i: (0, 0)),
            pl.BlockSpec(memory_space=pltpu.SMEM),
            pl.BlockSpec((parts * count, block, times), lambda i: (0, i, 0)),
        ],
        out_specs=pl.BlockSpec((parts * count, block, times), lambda i: (0, i, 0)),
        out_shape=jax.ShapeDtypeStruct((parts * count, rows, times), jnp.bfloat16),
    )(table, station_gain, flat)
    return out.reshape(count, parts, rows, times)


def beam_kernel(x_ref, w_ref, o_ref):
    stations = w_ref.shape[1]
    xt = x_ref[...].T
    x_real = xt[:, :stations]
    x_imag = xt[:, stations:]
    w_real = w_ref[0]
    w_imag = w_ref[1]
    f32 = jnp.float32
    beam_real = jnp.dot(x_real, w_real, preferred_element_type=f32) + jnp.dot(
        x_imag, w_imag, preferred_element_type=f32
    )
    beam_imag = jnp.dot(x_imag, w_real, preferred_element_type=f32) - jnp.dot(
        x_real, w_imag, preferred_element_type=f32
    )
    o_ref[:, 0, :] = beam_real.astype(o_ref.dtype)
    o_ref[:, 1, :] = beam_imag.astype(o_ref.dtype)


def beamform(stacked, weights):
    chans, rows, times = stacked.shape
    stations, beams = weights.shape[2], weights.shape[3]
    block = 1024 if times % 1024 == 0 else times
    return pl.pallas_call(
        beam_kernel,
        grid=(chans, times // block),
        in_specs=[
            pl.BlockSpec((None, rows, block), lambda c, t: (c, 0, t)),
            pl.BlockSpec((None, 2, stations, beams), lambda c, t: (c, 0, 0, 0)),
        ],
        out_specs=pl.BlockSpec((None, block, 2, beams), lambda c, t: (c, t, 0, 0)),
        out_shape=jax.ShapeDtypeStruct((chans, times, 2, beams), jnp.bfloat16),
    )(stacked, weights)


def local(samples, station_gain, station_map, steer_phase):
    count = samples.shape[1]
    row_count = samples.shape[2]
    spec_count = samples.shape[3]
    chan_size = lax.axis_size("chan")
    tm_size = lax.axis_size("tm")
    spectra = channelize(dft_table(count), samples, station_gain)
    split_channels = (count // chan_size) % tm_size == 0
    if split_channels:
        phase = exchange_phase(steer_phase, tm_size)
        spectra, phase = lax.optimization_barrier((spectra, phase))
    else:
        phase = steer_phase
    owned = lax.all_to_all(spectra, "chan", split_axis=0, concat_axis=2, tiled=True)
    chans = owned.shape[0]
    stations = owned.shape[2]
    stacked = owned.reshape(chans, 2 * stations, spec_count)
    spectra_total = spec_count * tm_size
    gram_sum = jnp.einsum("cat,cbt->cab", stacked, stacked, preferred_element_type=jnp.float32)
    part_real = gram_sum[:, :stations, :stations] + gram_sum[:, stations:, stations:]
    part_imag = gram_sum[:, stations:, :stations] - gram_sum[:, :stations, stations:]
    upper = jnp.arange(stations)[:, None] <= jnp.arange(stations)[None, :]
    if split_channels:
        part = jnp.where(upper, part_real, part_imag).astype(jnp.bfloat16)
    else:
        part = jnp.concatenate((part_real, part_imag), axis=1).astype(jnp.bfloat16)
    if split_channels:
        cov = lax.psum_scatter(part, "tm", scatter_dimension=0, tiled=True).astype(jnp.float32)
    else:
        cov = lax.psum(part, "tm").astype(jnp.float32)
    cov = cov / spectra_total
    if split_channels:
        cov_real = jnp.where(upper, cov, jnp.swapaxes(cov, 1, 2))
        below = jnp.where(upper, 0.0, cov)
        cov_imag = below - jnp.swapaxes(below, 1, 2)
        cov = jnp.concatenate((cov_real, cov_imag), axis=1)
    phase_rows = jnp.take(phase, station_map, axis=1)
    weights = chebyshev(
        cov[:, :stations], cov[:, stations:], jnp.cos(phase_rows), jnp.sin(phase_rows)
    )
    if split_channels:
        weights = lax.all_gather(weights, "tm", axis=0, tiled=True)
    else:
        weights = lax.all_gather(weights, "tm", axis=3, tiled=True)
    return beamform(stacked, weights)


def solution(mesh):
    in_specs = (
        P(None, None, ("groups", "chan"), "tm"),
        P(("groups", "chan")),
        P("groups"),
        P("chan", None, ("groups", "tm")),
    )
    out_specs = P("chan", "tm", None, "groups")
    return jax.shard_map(local, mesh=mesh, in_specs=in_specs, out_specs=out_specs, check_vma=False)
```

```python
import math

import jax
import jax.numpy as jnp
from jax import lax
from jax.experimental import pallas as pl
from jax.experimental.pallas import tpu as pltpu
from jax.sharding import PartitionSpec as P

ITERS = 8


def dft_table(count):
    index = jnp.arange(count, dtype=jnp.int32)
    turns = (index[:, None] * index[None, :] % count).astype(jnp.float32)
    angle_grid = 2.0 * math.pi * turns / count
    cosine = jnp.cos(angle_grid)
    sine = jnp.sin(angle_grid)
    upper = jnp.concatenate((cosine, sine), axis=1)
    lower = jnp.concatenate((-sine, cosine), axis=1)
    table = jnp.concatenate((upper, lower), axis=0).astype(jnp.bfloat16)
    return table.reshape(2, count, 2 * count).transpose(1, 0, 2).reshape(2 * count, 2 * count)


def chebyshev(cov_real, cov_imag, steer_real, steer_imag):
    high = lax.Precision.HIGH
    stations = cov_real.shape[1]
    eye = jnp.eye(stations, dtype=jnp.float32)
    loading = jnp.sum(jnp.where(eye > 0, cov_real, 0.0), axis=(1, 2)) / stations
    row_mass = jnp.sum(jnp.sqrt(cov_real * cov_real + cov_imag * cov_imag), axis=2)
    bound = loading + jnp.max(row_mass, axis=1)
    center = ((bound + loading) / 2.0)[:, None, None]
    radius = ((bound - loading) / 2.0)[:, None, None]
    loaded = cov_real + loading[:, None, None] * eye
    block = jnp.concatenate(
        (
            jnp.concatenate((loaded, -cov_imag), axis=2),
            jnp.concatenate((cov_imag, loaded), axis=2),
        ),
        axis=1,
    )
    steer = jnp.concatenate((steer_real, steer_imag), axis=1)
    res = steer
    dirn = res / center
    sol = jnp.zeros_like(steer)
    rho = radius / center

    def body(_, carry):
        sol, res, dirn, rho = carry
        sol = sol + dirn
        img = jnp.einsum("cjk,ckb->cjb", block, dirn, precision=high)
        res = res - img
        rho_next = 1.0 / (2.0 * center / radius - rho)
        dirn = rho_next * rho * dirn + 2.0 * rho_next / radius * res
        return sol, res, dirn, rho_next

    sol, _, _, _ = lax.fori_loop(0, ITERS, body, (sol, res, dirn, rho), unroll=True)
    response = jnp.sum(steer * sol, axis=1, keepdims=True)
    weights = (sol / response).astype(jnp.bfloat16)
    return weights.reshape(weights.shape[0], 2, stations, weights.shape[2])


def exchange_phase(steer_phase, tm_size):
    own = lax.axis_index("tm")
    block = steer_phase.shape[0] // tm_size
    pieces = steer_phase.reshape(tm_size, block, *steer_phase.shape[1:])
    received = [lax.dynamic_index_in_dim(pieces, own, 0, keepdims=False)]
    for shift in range(1, tm_size):
        target = (own + shift) % tm_size
        outgoing = lax.dynamic_index_in_dim(pieces, target, 0, keepdims=False)
        perm = [(j, (j + shift) % tm_size) for j in range(tm_size)]
        received.append(lax.ppermute(outgoing, "tm", perm))
    stacked = jnp.stack(received, axis=0)
    order = (own - jnp.arange(tm_size)) % tm_size
    ordered = jnp.take(stacked, order, axis=0)
    return jnp.moveaxis(ordered, 0, 2).reshape(block, steer_phase.shape[1], -1)


def dft_kernel(t_ref, g_ref, x_ref, o_ref):
    rows, times = x_ref.shape[1], x_ref.shape[2]
    base = pl.program_id(0) * rows
    wide = jnp.concatenate([x_ref[:, row, :] for row in range(rows)], axis=1)
    y = jnp.dot(t_ref[...], wide, preferred_element_type=jnp.float32)
    for row in range(rows):
        piece = y[:, row * times : (row + 1) * times]
        o_ref[:, row, :] = (piece * g_ref[base + row]).astype(o_ref.dtype)


def channelize(table, samples, station_gain):
    parts, count, rows, times = samples.shape
    flat = samples.reshape(parts * count, rows, times)
    block = 16 if rows % 16 == 0 else rows
    out = pl.pallas_call(
        dft_kernel,
        grid=(rows // block,),
        in_specs=[
            pl.BlockSpec((parts * count, parts * count), lambda i: (0, 0)),
            pl.BlockSpec(memory_space=pltpu.SMEM),
            pl.BlockSpec((parts * count, block, times), lambda i: (0, i, 0)),
        ],
        out_specs=pl.BlockSpec((parts * count, block, times), lambda i: (0, i, 0)),
        out_shape=jax.ShapeDtypeStruct((parts * count, rows, times), jnp.bfloat16),
    )(table, station_gain, flat)
    return out.reshape(count, parts, rows, times)


def beam_kernel(x_ref, w_ref, o_ref):
    stations = w_ref.shape[1]
    xt = x_ref[...].T
    x_real = xt[:, :stations]
    x_imag = xt[:, stations:]
    w_real = w_ref[0]
    w_imag = w_ref[1]
    f32 = jnp.float32
    beam_real = jnp.dot(x_real, w_real, preferred_element_type=f32) + jnp.dot(
        x_imag, w_imag, preferred_element_type=f32
    )
    beam_imag = jnp.dot(x_imag, w_real, preferred_element_type=f32) - jnp.dot(
        x_real, w_imag, preferred_element_type=f32
    )
    o_ref[:, 0, :] = beam_real.astype(o_ref.dtype)
    o_ref[:, 1, :] = beam_imag.astype(o_ref.dtype)


def beamform(stacked, weights):
    chans, rows, times = stacked.shape
    stations, beams = weights.shape[2], weights.shape[3]
    block = 1024 if times % 1024 == 0 else times
    return pl.pallas_call(
        beam_kernel,
        grid=(chans, times // block),
        in_specs=[
            pl.BlockSpec((None, rows, block), lambda c, t: (c, 0, t)),
            pl.BlockSpec((None, 2, stations, beams), lambda c, t: (c, 0, 0, 0)),
        ],
        out_specs=pl.BlockSpec((None, block, 2, beams), lambda c, t: (c, t, 0, 0)),
        out_shape=jax.ShapeDtypeStruct((chans, times, 2, beams), jnp.bfloat16),
    )(stacked, weights)


def local(samples, station_gain, station_map, steer_phase):
    count = samples.shape[1]
    row_count = samples.shape[2]
    spec_count = samples.shape[3]
    chan_size = lax.axis_size("chan")
    tm_size = lax.axis_size("tm")
    spectra = channelize(dft_table(count), samples, station_gain)
    split_channels = (count // chan_size) % tm_size == 0
    if split_channels:
        phase = exchange_phase(steer_phase, tm_size)
        spectra, phase = lax.optimization_barrier((spectra, phase))
    else:
        phase = steer_phase
    owned = lax.all_to_all(spectra, "chan", split_axis=0, concat_axis=2, tiled=True)
    chans = owned.shape[0]
    stations = owned.shape[2]
    stacked = owned.reshape(chans, 2 * stations, spec_count)
    spectra_total = spec_count * tm_size
    gram_sum = jnp.einsum("cat,cbt->cab", stacked, stacked, preferred_element_type=jnp.float32)
    part_real = gram_sum[:, :stations, :stations] + gram_sum[:, stations:, stations:]
    part_imag = gram_sum[:, stations:, :stations] - gram_sum[:, :stations, stations:]
    upper = jnp.arange(stations)[:, None] <= jnp.arange(stations)[None, :]
    if split_channels:
        part = jnp.where(upper, part_real, part_imag).astype(jnp.bfloat16)
    else:
        part = jnp.concatenate((part_real, part_imag), axis=1).astype(jnp.bfloat16)
    if split_channels:
        cov = lax.psum_scatter(part, "tm", scatter_dimension=0, tiled=True).astype(jnp.float32)
    else:
        cov = lax.psum(part, "tm").astype(jnp.float32)
    cov = cov / spectra_total
    if split_channels:
        cov_real = jnp.where(upper, cov, jnp.swapaxes(cov, 1, 2))
        below = jnp.where(upper, 0.0, cov)
        cov_imag = below - jnp.swapaxes(below, 1, 2)
        cov = jnp.concatenate((cov_real, cov_imag), axis=1)
    phase_rows = jnp.take(phase, station_map, axis=1)
    weights = chebyshev(
        cov[:, :stations], cov[:, stations:], jnp.cos(phase_rows), jnp.sin(phase_rows)
    )
    if split_channels:
        weights = lax.all_gather(weights, "tm", axis=0, tiled=True)
    else:
        weights = lax.all_gather(weights, "tm", axis=3, tiled=True)
    return beamform(stacked, weights)


def solution(mesh):
    in_specs = (
        P(None, None, ("groups", "chan"), "tm"),
        P(("groups", "chan")),
        P("groups"),
        P("chan", None, ("groups", "tm")),
    )
    out_specs = P("chan", "tm", None, "groups")
    return jax.shard_map(local, mesh=mesh, in_specs=in_specs, out_specs=out_specs, check_vma=False)
```

```python
import math

import jax
import jax.numpy as jnp
from jax import lax
from jax.experimental import pallas as pl
from jax.experimental.pallas import tpu as pltpu
from jax.sharding import PartitionSpec as P

ITERS = 8


def dft_table(count):
    index = jnp.arange(count, dtype=jnp.int32)
    turns = (index[:, None] * index[None, :] % count).astype(jnp.float32)
    angle_grid = 2.0 * math.pi * turns / count
    cosine = jnp.cos(angle_grid)
    sine = jnp.sin(angle_grid)
    upper = jnp.concatenate((cosine, sine), axis=1)
    lower = jnp.concatenate((-sine, cosine), axis=1)
    table = jnp.concatenate((upper, lower), axis=0).astype(jnp.bfloat16)
    return table.reshape(2, count, 2 * count).transpose(1, 0, 2).reshape(2 * count, 2 * count)


def chebyshev(cov_real, cov_imag, steer_real, steer_imag):
    high = lax.Precision.HIGH
    stations = cov_real.shape[1]
    eye = jnp.eye(stations, dtype=jnp.float32)
    loading = jnp.sum(jnp.where(eye > 0, cov_real, 0.0), axis=(1, 2)) / stations
    row_mass = jnp.sum(jnp.sqrt(cov_real * cov_real + cov_imag * cov_imag), axis=2)
    bound = loading + jnp.max(row_mass, axis=1)
    center = ((bound + loading) / 2.0)[:, None, None]
    radius = ((bound - loading) / 2.0)[:, None, None]
    loaded = cov_real + loading[:, None, None] * eye
    block = jnp.concatenate(
        (
            jnp.concatenate((loaded, -cov_imag), axis=2),
            jnp.concatenate((cov_imag, loaded), axis=2),
        ),
        axis=1,
    )
    steer = jnp.concatenate((steer_real, steer_imag), axis=1)
    res = steer
    dirn = res / center
    sol = jnp.zeros_like(steer)
    rho = radius / center

    def body(_, carry):
        sol, res, dirn, rho = carry
        sol = sol + dirn
        img = jnp.einsum("cjk,ckb->cjb", block, dirn, precision=high)
        res = res - img
        rho_next = 1.0 / (2.0 * center / radius - rho)
        dirn = rho_next * rho * dirn + 2.0 * rho_next / radius * res
        return sol, res, dirn, rho_next

    sol, _, _, _ = lax.fori_loop(0, ITERS, body, (sol, res, dirn, rho), unroll=True)
    response = jnp.sum(steer * sol, axis=1, keepdims=True)
    weights = (sol / response).astype(jnp.bfloat16)
    return weights.reshape(weights.shape[0], 2, stations, weights.shape[2])


def exchange_phase(steer_phase, tm_size):
    own = lax.axis_index("tm")
    block = steer_phase.shape[0] // tm_size
    pieces = steer_phase.reshape(tm_size, block, *steer_phase.shape[1:])
    received = [lax.dynamic_index_in_dim(pieces, own, 0, keepdims=False)]
    for shift in range(1, tm_size):
        target = (own + shift) % tm_size
        outgoing = lax.dynamic_index_in_dim(pieces, target, 0, keepdims=False)
        perm = [(j, (j + shift) % tm_size) for j in range(tm_size)]
        received.append(lax.ppermute(outgoing, "tm", perm))
    stacked = jnp.stack(received, axis=0)
    order = (own - jnp.arange(tm_size)) % tm_size
    ordered = jnp.take(stacked, order, axis=0)
    return jnp.moveaxis(ordered, 0, 2).reshape(block, steer_phase.shape[1], -1)


def dft_kernel(t_ref, g_ref, x_ref, o_ref):
    base = pl.program_id(0) * x_ref.shape[1]
    table = t_ref[...]
    rows = []
    for row in range(x_ref.shape[1]):
        y = jnp.dot(table, x_ref[:, row, :], preferred_element_type=jnp.float32)
        rows.append(y * g_ref[base + row])
    o_ref[...] = jnp.stack(rows, axis=1).astype(o_ref.dtype)


def channelize(table, samples, station_gain):
    parts, count, rows, times = samples.shape
    flat = samples.reshape(parts * count, rows, times)
    block = 16 if rows % 16 == 0 else rows
    out = pl.pallas_call(
        dft_kernel,
        grid=(rows // block,),
        in_specs=[
            pl.BlockSpec((parts * count, parts * count), lambda i: (0, 0)),
            pl.BlockSpec(memory_space=pltpu.SMEM),
            pl.BlockSpec((parts * count, block, times), lambda i: (0, i, 0)),
        ],
        out_specs=pl.BlockSpec((parts * count, block, times), lambda i: (0, i, 0)),
        out_shape=jax.ShapeDtypeStruct((parts * count, rows, times), jnp.bfloat16),
    )(table, station_gain, flat)
    return out.reshape(count, parts, rows, times)


def beam_kernel(x_ref, w_ref, o_ref):
    stations = w_ref.shape[1]
    xt = x_ref[...].T
    x_real = xt[:, :stations]
    x_imag = xt[:, stations:]
    w_real = w_ref[0]
    w_imag = w_ref[1]
    f32 = jnp.float32
    beam_real = jnp.dot(x_real, w_real, preferred_element_type=f32) + jnp.dot(
        x_imag, w_imag, preferred_element_type=f32
    )
    beam_imag = jnp.dot(x_imag, w_real, preferred_element_type=f32) - jnp.dot(
        x_real, w_imag, preferred_element_type=f32
    )
    o_ref[:, 0, :] = beam_real.astype(o_ref.dtype)
    o_ref[:, 1, :] = beam_imag.astype(o_ref.dtype)


def beamform(stacked, weights):
    chans, rows, times = stacked.shape
    stations, beams = weights.shape[2], weights.shape[3]
    block = 1024 if times % 1024 == 0 else times
    return pl.pallas_call(
        beam_kernel,
        grid=(chans, times // block),
        in_specs=[
            pl.BlockSpec((None, rows, block), lambda c, t: (c, 0, t)),
            pl.BlockSpec((None, 2, stations, beams), lambda c, t: (c, 0, 0, 0)),
        ],
        out_specs=pl.BlockSpec((None, block, 2, beams), lambda c, t: (c, t, 0, 0)),
        out_shape=jax.ShapeDtypeStruct((chans, times, 2, beams), jnp.bfloat16),
    )(stacked, weights)


def local(samples, station_gain, station_map, steer_phase):
    count = samples.shape[1]
    row_count = samples.shape[2]
    spec_count = samples.shape[3]
    chan_size = lax.axis_size("chan")
    tm_size = lax.axis_size("tm")
    spectra = channelize(dft_table(count), samples, station_gain)
    split_channels = (count // chan_size) % tm_size == 0
    if split_channels:
        phase = exchange_phase(steer_phase, tm_size)
        spectra, phase = lax.optimization_barrier((spectra, phase))
    else:
        phase = steer_phase
    owned = lax.all_to_all(spectra, "chan", split_axis=0, concat_axis=2, tiled=True)
    chans = owned.shape[0]
    stations = owned.shape[2]
    stacked = owned.reshape(chans, 2 * stations, spec_count)
    spectra_total = spec_count * tm_size
    gram_sum = jnp.einsum("cat,cbt->cab", stacked, stacked, preferred_element_type=jnp.float32)
    part_real = gram_sum[:, :stations, :stations] + gram_sum[:, stations:, stations:]
    part_imag = gram_sum[:, stations:, :stations] - gram_sum[:, :stations, stations:]
    upper = jnp.arange(stations)[:, None] <= jnp.arange(stations)[None, :]
    if split_channels:
        part = jnp.where(upper, part_real, part_imag).astype(jnp.bfloat16)
    else:
        part = jnp.concatenate((part_real, part_imag), axis=1).astype(jnp.bfloat16)
    if split_channels:
        cov = lax.psum_scatter(part, "tm", scatter_dimension=0, tiled=True).astype(jnp.float32)
    else:
        cov = lax.psum(part, "tm").astype(jnp.float32)
    cov = cov / spectra_total
    if split_channels:
        cov_real = jnp.where(upper, cov, jnp.swapaxes(cov, 1, 2))
        below = jnp.where(upper, 0.0, cov)
        cov_imag = below - jnp.swapaxes(below, 1, 2)
        cov = jnp.concatenate((cov_real, cov_imag), axis=1)
    phase_rows = jnp.take(phase, station_map, axis=1)
    weights = chebyshev(
        cov[:, :stations], cov[:, stations:], jnp.cos(phase_rows), jnp.sin(phase_rows)
    )
    if split_channels:
        weights = lax.all_gather(weights, "tm", axis=0, tiled=True)
    else:
        weights = lax.all_gather(weights, "tm", axis=3, tiled=True)
    return beamform(stacked, weights)


def solution(mesh):
    in_specs = (
        P(None, None, ("groups", "chan"), "tm"),
        P(("groups", "chan")),
        P("groups"),
        P("chan", None, ("groups", "tm")),
    )
    out_specs = P("chan", "tm", None, "groups")
    return jax.shard_map(local, mesh=mesh, in_specs=in_specs, out_specs=out_specs, check_vma=False)
```

```python
import math

import jax
import jax.numpy as jnp
from jax import lax
from jax.experimental import pallas as pl
from jax.experimental.pallas import tpu as pltpu
from jax.sharding import PartitionSpec as P

ITERS = 8


def dft_table(count):
    index = jnp.arange(count, dtype=jnp.int32)
    turns = (index[:, None] * index[None, :] % count).astype(jnp.float32)
    angle_grid = 2.0 * math.pi * turns / count
    cosine = jnp.cos(angle_grid)
    sine = jnp.sin(angle_grid)
    upper = jnp.concatenate((cosine, sine), axis=1)
    lower = jnp.concatenate((-sine, cosine), axis=1)
    table = jnp.concatenate((upper, lower), axis=0).astype(jnp.bfloat16)
    return table.reshape(2, count, 2 * count).transpose(1, 0, 2).reshape(2 * count, 2 * count)


def chebyshev(cov_real, cov_imag, steer_real, steer_imag):
    high = lax.Precision.HIGH
    stations = cov_real.shape[1]
    eye = jnp.eye(stations, dtype=jnp.float32)
    loading = jnp.sum(jnp.where(eye > 0, cov_real, 0.0), axis=(1, 2)) / stations
    row_mass = jnp.sum(jnp.sqrt(cov_real * cov_real + cov_imag * cov_imag), axis=2)
    bound = loading + jnp.max(row_mass, axis=1)
    center = ((bound + loading) / 2.0)[:, None, None]
    radius = ((bound - loading) / 2.0)[:, None, None]
    loaded = cov_real + loading[:, None, None] * eye
    block = jnp.concatenate(
        (
            jnp.concatenate((loaded, -cov_imag), axis=2),
            jnp.concatenate((cov_imag, loaded), axis=2),
        ),
        axis=1,
    )
    steer = jnp.concatenate((steer_real, steer_imag), axis=1)
    res = steer
    dirn = res / center
    sol = jnp.zeros_like(steer)
    rho = radius / center

    def body(_, carry):
        sol, res, dirn, rho = carry
        sol = sol + dirn
        img = jnp.einsum("cjk,ckb->cjb", block, dirn, precision=high)
        res = res - img
        rho_next = 1.0 / (2.0 * center / radius - rho)
        dirn = rho_next * rho * dirn + 2.0 * rho_next / radius * res
        return sol, res, dirn, rho_next

    sol, _, _, _ = lax.fori_loop(0, ITERS, body, (sol, res, dirn, rho), unroll=True)
    response = jnp.sum(steer * sol, axis=1, keepdims=True)
    weights = (sol / response).astype(jnp.bfloat16)
    return weights.reshape(weights.shape[0], 2, stations, weights.shape[2])


def exchange_phase(steer_phase, tm_size):
    own = lax.axis_index("tm")
    block = steer_phase.shape[0] // tm_size
    pieces = steer_phase.reshape(tm_size, block, *steer_phase.shape[1:])
    received = [lax.dynamic_index_in_dim(pieces, own, 0, keepdims=False)]
    for shift in range(1, tm_size):
        target = (own + shift) % tm_size
        outgoing = lax.dynamic_index_in_dim(pieces, target, 0, keepdims=False)
        perm = [(j, (j + shift) % tm_size) for j in range(tm_size)]
        received.append(lax.ppermute(outgoing, "tm", perm))
    stacked = jnp.stack(received, axis=0)
    order = (own - jnp.arange(tm_size)) % tm_size
    ordered = jnp.take(stacked, order, axis=0)
    return jnp.moveaxis(ordered, 0, 2).reshape(block, steer_phase.shape[1], -1)


def dft_kernel(t_ref, g_ref, x_ref, o_ref):
    base = pl.program_id(0) * x_ref.shape[1]
    table = t_ref[...]
    for row in range(x_ref.shape[1]):
        y = jnp.dot(table, x_ref[:, row, :], preferred_element_type=jnp.float32)
        o_ref[:, row, :] = (y * g_ref[base + row]).astype(o_ref.dtype)


def channelize(table, samples, station_gain):
    parts, count, rows, times = samples.shape
    flat = samples.reshape(parts * count, rows, times)
    block = 16 if rows % 16 == 0 else rows
    out = pl.pallas_call(
        dft_kernel,
        grid=(rows // block,),
        in_specs=[
            pl.BlockSpec((parts * count, parts * count), lambda i: (0, 0)),
            pl.BlockSpec(memory_space=pltpu.SMEM),
            pl.BlockSpec((parts * count, block, times), lambda i: (0, i, 0)),
        ],
        out_specs=pl.BlockSpec((parts * count, block, times), lambda i: (0, i, 0)),
        out_shape=jax.ShapeDtypeStruct((parts * count, rows, times), jnp.bfloat16),
    )(table, station_gain, flat)
    return out.reshape(count, parts, rows, times)


def beam_kernel(x_ref, w_ref, o_ref):
    stations = w_ref.shape[1]
    x_real = x_ref[:stations, :]
    x_imag = x_ref[stations:, :]
    w_real = w_ref[0]
    w_imag = w_ref[1]

    def product(x, w):
        return lax.dot_general(
            x, w, (((0,), (0,)), ((), ())), preferred_element_type=jnp.float32
        )

    beam_real = product(x_real, w_real) + product(x_imag, w_imag)
    beam_imag = product(x_imag, w_real) - product(x_real, w_imag)
    o_ref[:, 0, :] = beam_real.astype(o_ref.dtype)
    o_ref[:, 1, :] = beam_imag.astype(o_ref.dtype)


def beamform(stacked, weights):
    chans, rows, times = stacked.shape
    stations, beams = weights.shape[2], weights.shape[3]
    block = 1024 if times % 1024 == 0 else times
    return pl.pallas_call(
        beam_kernel,
        grid=(chans, times // block),
        in_specs=[
            pl.BlockSpec((None, rows, block), lambda c, t: (c, 0, t)),
            pl.BlockSpec((None, 2, stations, beams), lambda c, t: (c, 0, 0, 0)),
        ],
        out_specs=pl.BlockSpec((None, block, 2, beams), lambda c, t: (c, t, 0, 0)),
        out_shape=jax.ShapeDtypeStruct((chans, times, 2, beams), jnp.bfloat16),
    )(stacked, weights)


def local(samples, station_gain, station_map, steer_phase):
    count = samples.shape[1]
    row_count = samples.shape[2]
    spec_count = samples.shape[3]
    chan_size = lax.axis_size("chan")
    tm_size = lax.axis_size("tm")
    spectra = channelize(dft_table(count), samples, station_gain)
    split_channels = (count // chan_size) % tm_size == 0
    if split_channels:
        phase = exchange_phase(steer_phase, tm_size)
        spectra, phase = lax.optimization_barrier((spectra, phase))
    else:
        phase = steer_phase
    owned = lax.all_to_all(spectra, "chan", split_axis=0, concat_axis=2, tiled=True)
    chans = owned.shape[0]
    stations = owned.shape[2]
    stacked = owned.reshape(chans, 2 * stations, spec_count)
    spectra_total = spec_count * tm_size
    gram_sum = jnp.einsum("cat,cbt->cab", stacked, stacked, preferred_element_type=jnp.float32)
    part_real = gram_sum[:, :stations, :stations] + gram_sum[:, stations:, stations:]
    part_imag = gram_sum[:, stations:, :stations] - gram_sum[:, :stations, stations:]
    upper = jnp.arange(stations)[:, None] <= jnp.arange(stations)[None, :]
    if split_channels:
        part = jnp.where(upper, part_real, part_imag).astype(jnp.bfloat16)
    else:
        part = jnp.concatenate((part_real, part_imag), axis=1).astype(jnp.bfloat16)
    if split_channels:
        cov = lax.psum_scatter(part, "tm", scatter_dimension=0, tiled=True).astype(jnp.float32)
    else:
        cov = lax.psum(part, "tm").astype(jnp.float32)
    cov = cov / spectra_total
    if split_channels:
        cov_real = jnp.where(upper, cov, jnp.swapaxes(cov, 1, 2))
        below = jnp.where(upper, 0.0, cov)
        cov_imag = below - jnp.swapaxes(below, 1, 2)
        cov = jnp.concatenate((cov_real, cov_imag), axis=1)
    phase_rows = jnp.take(phase, station_map, axis=1)
    weights = chebyshev(
        cov[:, :stations], cov[:, stations:], jnp.cos(phase_rows), jnp.sin(phase_rows)
    )
    if split_channels:
        weights = lax.all_gather(weights, "tm", axis=0, tiled=True)
    else:
        weights = lax.all_gather(weights, "tm", axis=3, tiled=True)
    return beamform(stacked, weights)


def solution(mesh):
    in_specs = (
        P(None, None, ("groups", "chan"), "tm"),
        P(("groups", "chan")),
        P("groups"),
        P("chan", None, ("groups", "tm")),
    )
    out_specs = P("chan", "tm", None, "groups")
    return jax.shard_map(local, mesh=mesh, in_specs=in_specs, out_specs=out_specs, check_vma=False)
```

```python
import math

import jax
import jax.numpy as jnp
from jax import lax
from jax.experimental import pallas as pl
from jax.experimental.pallas import tpu as pltpu
from jax.sharding import PartitionSpec as P

ITERS = 8


def dft_table(count):
    index = jnp.arange(count, dtype=jnp.int32)
    turns = (index[:, None] * index[None, :] % count).astype(jnp.float32)
    angle_grid = 2.0 * math.pi * turns / count
    cosine = jnp.cos(angle_grid)
    sine = jnp.sin(angle_grid)
    upper = jnp.concatenate((cosine, sine), axis=1)
    lower = jnp.concatenate((-sine, cosine), axis=1)
    table = jnp.concatenate((upper, lower), axis=0).astype(jnp.bfloat16)
    return table.reshape(2, count, 2 * count).transpose(1, 0, 2).reshape(2 * count, 2 * count)


def chebyshev(cov_real, cov_imag, steer_real, steer_imag):
    high = lax.Precision.HIGH
    stations = cov_real.shape[1]
    eye = jnp.eye(stations, dtype=jnp.float32)
    loading = jnp.sum(jnp.where(eye > 0, cov_real, 0.0), axis=(1, 2)) / stations
    row_mass = jnp.sum(jnp.sqrt(cov_real * cov_real + cov_imag * cov_imag), axis=2)
    bound = loading + jnp.max(row_mass, axis=1)
    center = ((bound + loading) / 2.0)[:, None, None]
    radius = ((bound - loading) / 2.0)[:, None, None]
    loaded = cov_real + loading[:, None, None] * eye
    block = jnp.concatenate(
        (
            jnp.concatenate((loaded, -cov_imag), axis=2),
            jnp.concatenate((cov_imag, loaded), axis=2),
        ),
        axis=1,
    )
    steer = jnp.concatenate((steer_real, steer_imag), axis=1)
    res = steer
    dirn = res / center
    sol = jnp.zeros_like(steer)
    rho = radius / center

    def body(_, carry):
        sol, res, dirn, rho = carry
        sol = sol + dirn
        img = jnp.einsum("cjk,ckb->cjb", block, dirn, precision=high)
        res = res - img
        rho_next = 1.0 / (2.0 * center / radius - rho)
        dirn = rho_next * rho * dirn + 2.0 * rho_next / radius * res
        return sol, res, dirn, rho_next

    sol, _, _, _ = lax.fori_loop(0, ITERS, body, (sol, res, dirn, rho), unroll=True)
    response = jnp.sum(steer * sol, axis=1, keepdims=True)
    weights = (sol / response).astype(jnp.bfloat16)
    return weights.reshape(weights.shape[0], 2, stations, weights.shape[2])


def dft_kernel(t_ref, g_ref, x_ref, o_ref):
    base = pl.program_id(0) * x_ref.shape[1]
    table = t_ref[...]
    for row in range(x_ref.shape[1]):
        y = jnp.dot(table, x_ref[:, row, :], preferred_element_type=jnp.float32)
        o_ref[:, row, :] = (y * g_ref[base + row]).astype(o_ref.dtype)


def channelize(table, samples, station_gain):
    parts, count, rows, times = samples.shape
    flat = samples.reshape(parts * count, rows, times)
    block = 16 if rows % 16 == 0 else rows
    out = pl.pallas_call(
        dft_kernel,
        grid=(rows // block,),
        in_specs=[
            pl.BlockSpec((parts * count, parts * count), lambda i: (0, 0)),
            pl.BlockSpec(memory_space=pltpu.SMEM),
            pl.BlockSpec((parts * count, block, times), lambda i: (0, i, 0)),
        ],
        out_specs=pl.BlockSpec((parts * count, block, times), lambda i: (0, i, 0)),
        out_shape=jax.ShapeDtypeStruct((parts * count, rows, times), jnp.bfloat16),
    )(table, station_gain, flat)
    return out.reshape(count, parts, rows, times)


def beam_kernel(x_ref, w_ref, o_ref):
    stations = w_ref.shape[1]
    xt = x_ref[...].T
    x_real = xt[:, :stations]
    x_imag = xt[:, stations:]
    w_real = w_ref[0]
    w_imag = w_ref[1]
    f32 = jnp.float32
    beam_real = jnp.dot(x_real, w_real, preferred_element_type=f32) + jnp.dot(
        x_imag, w_imag, preferred_element_type=f32
    )
    beam_imag = jnp.dot(x_imag, w_real, preferred_element_type=f32) - jnp.dot(
        x_real, w_imag, preferred_element_type=f32
    )
    o_ref[:, 0, :] = beam_real.astype(o_ref.dtype)
    o_ref[:, 1, :] = beam_imag.astype(o_ref.dtype)


def beamform(stacked, weights):
    chans, rows, times = stacked.shape
    stations, beams = weights.shape[2], weights.shape[3]
    block = 1024 if times % 1024 == 0 else times
    return pl.pallas_call(
        beam_kernel,
        grid=(chans, times // block),
        in_specs=[
            pl.BlockSpec((None, rows, block), lambda c, t: (c, 0, t)),
            pl.BlockSpec((None, 2, stations, beams), lambda c, t: (c, 0, 0, 0)),
        ],
        out_specs=pl.BlockSpec((None, block, 2, beams), lambda c, t: (c, t, 0, 0)),
        out_shape=jax.ShapeDtypeStruct((chans, times, 2, beams), jnp.bfloat16),
    )(stacked, weights)


def local(samples, station_gain, station_map, steer_phase):
    count = samples.shape[1]
    row_count = samples.shape[2]
    spec_count = samples.shape[3]
    chan_size = lax.axis_size("chan")
    tm_size = lax.axis_size("tm")
    spectra = channelize(dft_table(count), samples, station_gain)
    split_channels = (count // chan_size) % tm_size == 0
    if split_channels:
        phase = lax.all_to_all(steer_phase, "tm", split_axis=0, concat_axis=2, tiled=True)
        spectra, phase = lax.optimization_barrier((spectra, phase))
    else:
        phase = steer_phase
    owned = lax.all_to_all(spectra, "chan", split_axis=0, concat_axis=2, tiled=True)
    chans = owned.shape[0]
    stations = owned.shape[2]
    stacked = owned.reshape(chans, 2 * stations, spec_count)
    spectra_total = spec_count * tm_size
    gram_sum = jnp.einsum("cat,cbt->cab", stacked, stacked, preferred_element_type=jnp.float32)
    part_real = gram_sum[:, :stations, :stations] + gram_sum[:, stations:, stations:]
    part_imag = gram_sum[:, stations:, :stations] - gram_sum[:, :stations, stations:]
    upper = jnp.arange(stations)[:, None] <= jnp.arange(stations)[None, :]
    if split_channels:
        part = jnp.where(upper, part_real, part_imag).astype(jnp.bfloat16)
    else:
        part = jnp.concatenate((part_real, part_imag), axis=1).astype(jnp.bfloat16)
    if split_channels:
        cov = lax.psum_scatter(part, "tm", scatter_dimension=0, tiled=True).astype(jnp.float32)
    else:
        cov = lax.psum(part, "tm").astype(jnp.float32)
    cov = cov / spectra_total
    if split_channels:
        cov_real = jnp.where(upper, cov, jnp.swapaxes(cov, 1, 2))
        below = jnp.where(upper, 0.0, cov)
        cov_imag = below - jnp.swapaxes(below, 1, 2)
        cov = jnp.concatenate((cov_real, cov_imag), axis=1)
    phase_rows = jnp.take(phase, station_map, axis=1)
    weights = chebyshev(
        cov[:, :stations], cov[:, stations:], jnp.cos(phase_rows), jnp.sin(phase_rows)
    )
    if split_channels:
        weights = lax.all_gather(weights, "tm", axis=0, tiled=True)
    else:
        weights = lax.all_gather(weights, "tm", axis=3, tiled=True)
    return beamform(stacked, weights)


def solution(mesh):
    in_specs = (
        P(None, None, ("groups", "chan"), "tm"),
        P(("groups", "chan")),
        P("groups"),
        P("chan", None, ("groups", "tm")),
    )
    out_specs = P("chan", "tm", None, "groups")
    return jax.shard_map(local, mesh=mesh, in_specs=in_specs, out_specs=out_specs, check_vma=False)
```
